512 devices in a mesh: seq: 64 (over x, z), tp: 8 (over y, core).
Axes of the slice: x: 4, y: 4, z: 16, core: 2. Of those that a mesh axis runs over, the one named last changes fastest.
Arguments:
- queries: bfloat16 [64, 4, 8192], P('seq', None, 'tp'), may hold values from -40 to 40
- new_keys: bfloat16 [64, 4, 1024], P('seq', None, 'tp'), may hold values from -6 to 6
- new_values: bfloat16 [64, 4, 1024], P('seq', None, 'tp'), may hold values from -6 to 6
- prefix_keys: bfloat16 [8, 12288, 1024], P(None, 'seq', 'tp'), may hold values from -8 to 8
- prefix_values: bfloat16 [8, 12288, 1024], P(None, 'seq', 'tp'), may hold values from -6 to 6
- page_keys: bfloat16 [1024, 64, 1024], P('seq', None, 'tp'), may hold values from -6 to 6
- page_values: bfloat16 [1024, 64, 1024], P('seq', None, 'tp'), may hold values from -6 to 6
- out_weight: bfloat16 [8192, 8192], P('tp', 'seq'), may hold values from -0.5 to 0.5
- group_of: int32 [64], replicated, may hold values from 0 to 7, as said below
- prefix_len: int32 [8], replicated, may hold values from 2 to 12288, as said below
- total_len: int32 [64], replicated, may hold values from 3 to 16384, as said below
- page_owner: int32 [1024], P('seq'), may hold values from 0 to 63, as said below
- page_slot: int32 [1024], P('seq'), may hold values from 0 to 63, as said below
- new_valid: int32 [64, 4], replicated, may hold values from 0 to 1, as said below
Outputs:
- attn_out: bfloat16 [256, 8192], P('tp', 'seq')
The draws below stay inside these ranges and needn't reach their ends.
Inputs may be any that keep to these rules, and one draw needn't show every extreme that they name: `group_of`: every one of the 8 groups has at least one request. `prefix_len`: some group's prefix holds exactly 12288 tokens. `page_owner`: every request owns at least one page and at most 64 pages; one request owns exactly 64. `page_slot`: the pages of one request carry the slots 0, 1, 2 and so on, each once. A request's pages are full except the one of its highest slot, which holds 1 to 64 tokens; total_len is its group's prefix length plus these tokens. `new_valid`: each row is a run of ones followed by zeros, and its first entry is one.
All inputs are finite; a program needn't handle non-finite values.
Results may differ from the reference program's by a relative error of at most 0.022.
Values may be sent and summed in bfloat16 or wider, within the bound.
No kernel may reach another device: no remote copies, remote signals or barrier semaphores. Data moves between devices by JAX's collectives and lax.ppermute only.
A program may use at most 192 MiB of HBM per device.

```python
import jax
import jax.numpy as jnp
from jax import lax

D = 8192
HEADS = 64
KV_HEADS = 8
HEAD_DIM = 128
HPK = 8
GROUPS = 8
NEW = 4
PAGE = 64
PAGE_DEV = 16
REQS = 64
PREFIX = 12288
PAGES = 1024
N_SEQ = 64


def request_order(key):
    return jax.random.permutation(jax.random.fold_in(key, 107), REQS).astype(jnp.int32)


def group_ids(key):
    folded = jax.random.fold_in(key, 101)
    key_extra, key_order = jax.random.split(folded)
    request_ids = jnp.arange(REQS, dtype=jnp.int32)
    extras = jax.random.randint(key_extra, (REQS,), 0, GROUPS)
    base_ids = jnp.where(request_ids < GROUPS, request_ids % GROUPS, extras)
    ordering = jax.random.permutation(key_order, REQS)
    return base_ids[ordering].astype(jnp.int32)


def prefix_lengths(key):
    folded = jax.random.fold_in(key, 103)
    lengths = jax.random.randint(folded, (GROUPS,), 2, PREFIX + 1)
    longest = group_ids(key)[request_order(key)[0]]
    return jnp.where(jnp.arange(GROUPS, dtype=jnp.int32) == longest, PREFIX, lengths).astype(jnp.int32)


def page_table(key):
    folded = jax.random.fold_in(key, 104)
    key_shuffle, key_tail = jax.random.split(folded)
    order = request_order(key)
    heavy_pages = min(4 * (PAGES // REQS), PAGES - REQS + 1)
    page_ids = jnp.arange(PAGES, dtype=jnp.int32)
    others = 1 + jnp.maximum(page_ids - heavy_pages, 0) % (REQS - 1)
    position = jnp.where(page_ids < heavy_pages, 0, others)
    owners = order[position]
    owners = owners[jax.random.permutation(key_shuffle, PAGES)].astype(jnp.int32)
    one_hot = (owners[:, None] == jnp.arange(REQS, dtype=jnp.int32)[None, :]).astype(jnp.int32)
    earlier = jnp.cumsum(one_hot, axis=0) - one_hot
    slot_ids = jnp.sum(earlier * one_hot, axis=1).astype(jnp.int32)
    counts = jnp.sum(one_hot, axis=0)
    tails = jax.random.randint(key_tail, (REQS,), 1, PAGE + 1)
    tails = jnp.where(jnp.arange(REQS, dtype=jnp.int32) == order[0], PAGE, tails)
    suffix = ((counts - 1) * PAGE + tails).astype(jnp.int32)
    return (owners, slot_ids, suffix)


def draw_group_of(key, part):
    return group_ids(key)


def draw_prefix_len(key, part):
    return prefix_lengths(key)


def draw_total_len(key, part):
    return (prefix_lengths(key)[group_ids(key)] + page_table(key)[2]).astype(jnp.int32)


def draw_page_owner(key, part):
    return page_table(key)[0]


def draw_page_slot(key, part):
    return page_table(key)[1]


def draw_new_valid(key, part):
    counts = jax.random.randint(jax.random.fold_in(key, 105), (REQS,), 1, NEW + 1)
    return (jnp.arange(NEW, dtype=jnp.int32)[None, :] < counts[:, None]).astype(jnp.int32)


def draw_queries(key, part):
    key_main = jax.random.fold_in(jax.random.fold_in(key, 1), 0)
    full_shape = (REQS, NEW, HEADS, HEAD_DIM)
    base = jax.random.normal(key_main, full_shape, jnp.float32)
    return base.reshape(REQS, NEW, HEADS * HEAD_DIM).astype(jnp.bfloat16)


def draw_prefix_keys(key, part):
    key_main = jax.random.fold_in(jax.random.fold_in(key, 2), 0)
    full_shape = (GROUPS, PREFIX, KV_HEADS, HEAD_DIM)
    base = jax.random.normal(key_main, full_shape, jnp.float32)
    return base.reshape(GROUPS, PREFIX, KV_HEADS * HEAD_DIM).astype(jnp.bfloat16)


def shard_levels(stream_key, extent, cuts, smallest, high):
    def one(dim, parts):
        steps = jax.random.uniform(jax.random.fold_in(jax.random.fold_in(stream_key, 6), dim), (parts,), jnp.float32, smallest / len(cuts), high / len(cuts))
        return jnp.repeat(jnp.exp(steps), extent[dim] // parts).reshape((-1,) + (1,) * (len(extent) - dim - 1))

    gain = one(*cuts[0])
    for cut in cuts[1:]:
        gain = gain * one(*cut)
    return gain


def centred(own_key, extent, width, limit, shards=(), kind=jnp.bfloat16):
    entries = width * jax.random.normal(own_key, extent, jnp.float32)
    if shards:
        entries = entries * shard_levels(own_key, extent, shards, -0.22, 0.18)
    return jnp.clip(entries, -limit, limit).astype(kind)


def setup_inputs(seed: int = 0) -> dict:
    key_of = jax.random.split(jax.random.key(seed), 15)
    queries = draw_queries(jax.random.fold_in(key_of[14], 71), 0)
    new_keys = centred(key_of[1], (REQS, NEW, KV_HEADS * HEAD_DIM), 1.0, 6.0, ((0, 64), (2, 8)))
    new_values = centred(key_of[2], (REQS, NEW, KV_HEADS * HEAD_DIM), 1.0, 6.0, ((0, 64), (2, 8)))
    prefix_keys = draw_prefix_keys(jax.random.fold_in(key_of[14], 71), 0)
    prefix_values = centred(key_of[4], (GROUPS, PREFIX, KV_HEADS * HEAD_DIM), 1.0, 6.0, ((1, 64), (2, 8)))
    page_keys = centred(key_of[5], (PAGES, PAGE, KV_HEADS * HEAD_DIM), 1.0, 6.0, ((0, 64), (2, 8)))
    page_values = centred(key_of[6], (PAGES, PAGE, KV_HEADS * HEAD_DIM), 1.0, 6.0, ((0, 64), (2, 8)))
    out_weight = centred(key_of[7], (HEADS * HEAD_DIM, D), HEAD_DIM ** -0.5, 0.5, ((0, 8), (1, 64)))
    group_of = draw_group_of(jax.random.fold_in(key_of[14], 71), 0)
    prefix_len = draw_prefix_len(jax.random.fold_in(key_of[14], 71), 0)
    total_len = draw_total_len(jax.random.fold_in(key_of[14], 71), 0)
    page_owner = draw_page_owner(jax.random.fold_in(key_of[14], 71), 0)
    page_slot = draw_page_slot(jax.random.fold_in(key_of[14], 71), 0)
    new_valid = draw_new_valid(jax.random.fold_in(key_of[14], 71), 0)
    return dict(queries=queries, new_keys=new_keys, new_values=new_values, prefix_keys=prefix_keys, prefix_values=prefix_values, page_keys=page_keys, page_values=page_values, out_weight=out_weight, group_of=group_of, prefix_len=prefix_len, total_len=total_len, page_owner=page_owner, page_slot=page_slot, new_valid=new_valid)


NEG = -1.0e30


def softmax_part(scores, key_mask):
    masked = jnp.where(key_mask, scores, NEG)
    row_peak = jnp.max(masked, axis=-1)
    weights = jnp.where(key_mask, jnp.exp(masked - row_peak[..., None]), 0.0)
    return row_peak, jnp.sum(weights, axis=-1), weights.astype(jnp.bfloat16)


def combine(first_part, second_part):
    peak_a, total_a, out_a = first_part
    peak_b, total_b, out_b = second_part
    top_peak = jnp.maximum(peak_a, peak_b)
    factor_a = jnp.exp(peak_a - top_peak)
    factor_b = jnp.exp(peak_b - top_peak)
    return (top_peak, total_a * factor_a + total_b * factor_b,
            out_a * factor_a[..., None] + out_b * factor_b[..., None])


def reference(queries, new_keys, new_values, prefix_keys, prefix_values, page_keys, page_values,
              out_weight, group_of, prefix_len, total_len, page_owner, page_slot, new_valid):
    score_scale = HEAD_DIM ** -0.5
    query_all = queries.reshape(REQS, NEW, KV_HEADS, HPK, HEAD_DIM).astype(jnp.float32)
    suffix_len = total_len - prefix_len[group_of]

    def prefix_one(request):
        group_idx = group_of[request]
        key_rows = lax.dynamic_index_in_dim(prefix_keys, group_idx, 0, keepdims=False)
        key_rows = key_rows.reshape(PREFIX, KV_HEADS, HEAD_DIM).astype(jnp.float32)
        value_rows = lax.dynamic_index_in_dim(prefix_values, group_idx, 0, keepdims=False)
        value_rows = value_rows.reshape(PREFIX, KV_HEADS, HEAD_DIM).astype(jnp.float32)
        query_row = lax.dynamic_index_in_dim(query_all, request, 0, keepdims=False)
        scores = jnp.einsum("jkhd,pkd->jkhp", query_row, key_rows) * score_scale
        live_keys = jnp.arange(PREFIX, dtype=jnp.int32) < prefix_len[group_idx]
        row_peak, row_total, weights = softmax_part(scores, live_keys)
        values = jnp.einsum("jkhp,pkd->jkhd", weights.astype(jnp.float32), value_rows)
        return row_peak, row_total, values

    prefix_part = lax.map(prefix_one, jnp.arange(REQS, dtype=jnp.int32))

    key_blocks = page_keys.reshape(N_SEQ, PAGE_DEV, PAGE, KV_HEADS, HEAD_DIM)
    value_blocks = page_values.reshape(N_SEQ, PAGE_DEV, PAGE, KV_HEADS, HEAD_DIM)
    owner_blocks = page_owner.reshape(N_SEQ, PAGE_DEV)
    slot_blocks = page_slot.reshape(N_SEQ, PAGE_DEV)

    def pages_one(page_block):
        key_rows, value_rows, owners, slot_ids = page_block
        page_queries = jnp.take(query_all, owners, axis=0)
        scores = jnp.einsum("pjkhd,pikd->pjkhi", page_queries, key_rows.astype(jnp.float32)) * score_scale
        offsets = slot_ids[:, None] * PAGE + jnp.arange(PAGE, dtype=jnp.int32)[None, :]
        live_keys = offsets < jnp.take(suffix_len, owners)[:, None]
        row_peak, row_total, weights = softmax_part(scores, live_keys[:, None, None, None, :])
        values = jnp.einsum("pjkhi,pikd->pjkhd", weights.astype(jnp.float32), value_rows.astype(jnp.float32))
        return row_peak, row_total, values

    page_peak, page_total, page_out = lax.map(pages_one, (key_blocks, value_blocks, owner_blocks, slot_blocks))
    page_peak = page_peak.reshape(PAGES, NEW, KV_HEADS, HPK)
    page_total = page_total.reshape(PAGES, NEW, KV_HEADS, HPK)
    page_out = page_out.reshape(PAGES, NEW, KV_HEADS, HPK, HEAD_DIM)
    suffix_peak = jnp.maximum(jax.ops.segment_max(page_peak, page_owner, num_segments=REQS), NEG)
    factor = jnp.exp(page_peak - suffix_peak[page_owner])
    suffix_total = jax.ops.segment_sum(page_total * factor, page_owner, num_segments=REQS)
    suffix_out = jax.ops.segment_sum(page_out * factor[..., None], page_owner, num_segments=REQS)
    suffix_part = (suffix_peak, suffix_total, suffix_out)

    keys_new = new_keys.reshape(REQS, NEW, KV_HEADS, HEAD_DIM).astype(jnp.float32)
    values_new = new_values.reshape(REQS, NEW, KV_HEADS, HEAD_DIM).astype(jnp.float32)
    scores = jnp.einsum("rjkhd,rikd->rjkhi", query_all, keys_new) * score_scale
    causal = jnp.arange(NEW, dtype=jnp.int32)[None, :] <= jnp.arange(NEW, dtype=jnp.int32)[:, None]
    key_mask = causal[None, :, None, None, :] & (new_valid[:, None, None, None, :] == 1)
    row_peak, row_total, weights = softmax_part(scores, key_mask)
    new_out = jnp.einsum("rjkhi,rikd->rjkhd", weights.astype(jnp.float32), values_new)
    new_part = (row_peak, row_total, new_out)

    final_peak, final_total, final_out = combine(combine(prefix_part, suffix_part), new_part)
    valid_rows = new_valid.astype(jnp.float32)[:, :, None, None, None]
    attention = (final_out / final_total[..., None] * valid_rows).astype(jnp.bfloat16)
    attention = attention.reshape(REQS * NEW, HEADS * HEAD_DIM)
    return jnp.dot(attention, out_weight, preferred_element_type=jnp.float32).astype(jnp.bfloat16)
```

```python
import jax
import jax.numpy as jnp
from jax import lax
from jax.sharding import PartitionSpec as P

HEAD_DIM = 128
HPK = 8
GROUPS = 8
NEW = 4


NEG = -1e30


def local(
    queries,
    new_keys,
    new_values,
    prefix_keys,
    prefix_values,
    page_keys,
    page_values,
    out_weight,
    group_of,
    prefix_len,
    total_len,
    page_owner,
    page_slot,
    new_valid,
):
    req_dev = queries.shape[0]
    seq_count = lax.axis_size("seq")
    requests = req_dev * seq_count
    kv_local = new_keys.shape[2] // HEAD_DIM
    heads_local = kv_local * HPK
    score_scale = HEAD_DIM ** (-0.5)
    seq_idx = lax.axis_index("seq")
    gathered = lax.all_gather(queries, "seq", axis=0, tiled=True)
    query_all = gathered.reshape(requests, NEW, kv_local, HPK, HEAD_DIM)

    group_hot = group_of[:, None] == jnp.arange(GROUPS, dtype=jnp.int32)[None, :]
    own_prefix = jnp.sum(jnp.where(group_hot, prefix_len[None, :], 0), axis=1)
    suffix_len = total_len - own_prefix

    pre_dev = prefix_keys.shape[1]
    page_count = page_keys.shape[0]
    page_len = page_keys.shape[1]
    keys = jnp.concatenate(
        [
            prefix_keys.reshape(GROUPS * pre_dev, kv_local, HEAD_DIM),
            page_keys.reshape(page_count * page_len, kv_local, HEAD_DIM),
            new_keys.reshape(req_dev * NEW, kv_local, HEAD_DIM),
        ],
        axis=0,
    )
    values = jnp.concatenate(
        [
            prefix_values.reshape(GROUPS * pre_dev, kv_local, HEAD_DIM),
            page_values.reshape(page_count * page_len, kv_local, HEAD_DIM),
            new_values.reshape(req_dev * NEW, kv_local, HEAD_DIM),
        ],
        axis=0,
    )

    req_ids = jnp.arange(requests, dtype=jnp.int32)
    positions = seq_idx * pre_dev + jnp.arange(pre_dev, dtype=jnp.int32)
    pre_live = positions[None, :] < prefix_len[:, None]
    pre_mask = group_hot[:, :, None] & pre_live[None, :, :]
    pre_mask = pre_mask.reshape(requests, 1, GROUPS * pre_dev)
    pre_mask = jnp.broadcast_to(pre_mask, (requests, NEW, GROUPS * pre_dev))
    owner_hot = req_ids[:, None] == page_owner[None, :]
    offsets = page_slot[:, None] * page_len + jnp.arange(page_len, dtype=jnp.int32)[None, :]
    page_live = offsets[None, :, :] < suffix_len[:, None, None]
    page_mask = (owner_hot[:, :, None] & page_live).reshape(requests, 1, page_count * page_len)
    page_mask = jnp.broadcast_to(page_mask, (requests, NEW, page_count * page_len))
    new_owner = seq_idx * req_dev + jnp.arange(req_dev, dtype=jnp.int32)
    tok = jnp.arange(NEW, dtype=jnp.int32)
    causal = tok[None, :] <= tok[:, None]
    new_live = new_valid == 1
    new_mask = (
        (req_ids[:, None, None, None] == new_owner[None, None, :, None])
        & causal[None, :, None, :]
        & new_live[:, None, None, :]
    ).reshape(requests, NEW, req_dev * NEW)
    key_mask = jnp.concatenate([pre_mask, page_mask, new_mask], axis=2)
    key_mask = key_mask[:, :, None, None, :]

    scores = (
        jnp.einsum("rjkhd,nkd->rjkhn", query_all, keys, preferred_element_type=jnp.float32)
        * score_scale
    )
    masked = jnp.where(key_mask, scores, NEG)
    row_peak = jnp.max(masked, axis=-1)
    weights = jnp.where(key_mask, jnp.exp(masked - row_peak[..., None]), 0.0)
    row_total = jnp.sum(weights, axis=-1)
    out = jnp.einsum(
        "rjkhn,nkd->rjkhd", weights.astype(jnp.bfloat16), values, preferred_element_type=jnp.float32
    )

    top_peak = lax.pmax(row_peak, "seq")
    factor = jnp.exp(row_peak - top_peak)
    final_total, final_out = lax.psum((row_total * factor, out * factor[..., None]), "seq")
    valid_rows = new_valid.astype(jnp.float32)[:, :, None, None, None]
    attention = (final_out / final_total[..., None] * valid_rows).astype(jnp.bfloat16)
    attention = attention.reshape(requests * NEW, heads_local * HEAD_DIM)
    terms = jnp.dot(attention, out_weight, preferred_element_type=jnp.float32)
    summed = lax.psum_scatter(terms.astype(jnp.bfloat16), "tp", scatter_dimension=0, tiled=True)
    return summed


def solution(mesh):
    placed = (
        P("seq", None, "tp"),
        P("seq", None, "tp"),
        P("seq", None, "tp"),
        P(None, "seq", "tp"),
        P(None, "seq", "tp"),
        P("seq", None, "tp"),
        P("seq", None, "tp"),
        P("tp", "seq"),
        P(),
        P(),
        P(),
        P("seq"),
        P("seq"),
        P(),
    )
    return jax.shard_map(
        local, mesh=mesh, in_specs=placed, out_specs=P("tp", "seq"), check_vma=False
    )
```

```python
import jax
import jax.numpy as jnp
from jax import lax
from jax.sharding import Mesh, PartitionSpec as P

HEAD_DIM = 128
HPK = 8
GROUPS = 8
NEW = 4


NEG = -1e30
SEQ = ("sx", "sz")


def gather_rows(block):
    block = lax.all_gather(block, "sz", axis=0, tiled=True)
    return lax.all_gather(block, "sx", axis=0, tiled=True)


def inner_size(devices):
    try:
        return len({d.coords[2] for d in devices})
    except Exception:
        return 1


def local(
    queries,
    new_keys,
    new_values,
    prefix_keys,
    prefix_values,
    page_keys,
    page_values,
    out_weight,
    group_of,
    prefix_len,
    total_len,
    page_owner,
    page_slot,
    new_valid,
):
    req_dev = queries.shape[0]
    seq_count = lax.axis_size(SEQ)
    requests = req_dev * seq_count
    kv_local = new_keys.shape[2] // HEAD_DIM
    heads_local = kv_local * HPK
    score_scale = HEAD_DIM ** (-0.5)
    seq_idx = lax.axis_index(SEQ)
    gathered = gather_rows(queries)
    query_all = gathered.reshape(requests, NEW, kv_local, HPK, HEAD_DIM)

    group_hot = group_of[:, None] == jnp.arange(GROUPS, dtype=jnp.int32)[None, :]
    own_prefix = jnp.sum(jnp.where(group_hot, prefix_len[None, :], 0), axis=1)
    suffix_len = total_len - own_prefix

    pre_dev = prefix_keys.shape[1]
    page_count = page_keys.shape[0]
    page_len = page_keys.shape[1]
    keys = jnp.concatenate(
        [
            prefix_keys.reshape(GROUPS * pre_dev, kv_local, HEAD_DIM),
            page_keys.reshape(page_count * page_len, kv_local, HEAD_DIM),
            new_keys.reshape(req_dev * NEW, kv_local, HEAD_DIM),
        ],
        axis=0,
    )
    values = jnp.concatenate(
        [
            prefix_values.reshape(GROUPS * pre_dev, kv_local, HEAD_DIM),
            page_values.reshape(page_count * page_len, kv_local, HEAD_DIM),
            new_values.reshape(req_dev * NEW, kv_local, HEAD_DIM),
        ],
        axis=0,
    )

    req_ids = jnp.arange(requests, dtype=jnp.int32)
    positions = seq_idx * pre_dev + jnp.arange(pre_dev, dtype=jnp.int32)
    pre_live = positions[None, :] < prefix_len[:, None]
    pre_mask = group_hot[:, :, None] & pre_live[None, :, :]
    pre_mask = pre_mask.reshape(requests, 1, GROUPS * pre_dev)
    pre_mask = jnp.broadcast_to(pre_mask, (requests, NEW, GROUPS * pre_dev))
    owner_hot = req_ids[:, None] == page_owner[None, :]
    offsets = page_slot[:, None] * page_len + jnp.arange(page_len, dtype=jnp.int32)[None, :]
    page_live = offsets[None, :, :] < suffix_len[:, None, None]
    page_mask = (owner_hot[:, :, None] & page_live).reshape(requests, 1, page_count * page_len)
    page_mask = jnp.broadcast_to(page_mask, (requests, NEW, page_count * page_len))
    new_owner = seq_idx * req_dev + jnp.arange(req_dev, dtype=jnp.int32)
    tok = jnp.arange(NEW, dtype=jnp.int32)
    causal = tok[None, :] <= tok[:, None]
    new_live = new_valid == 1
    new_mask = (
        (req_ids[:, None, None, None] == new_owner[None, None, :, None])
        & causal[None, :, None, :]
        & new_live[:, None, None, :]
    ).reshape(requests, NEW, req_dev * NEW)
    key_mask = jnp.concatenate([pre_mask, page_mask, new_mask], axis=2)
    key_mask = key_mask[:, :, None, None, :]

    scores = (
        jnp.einsum("rjkhd,nkd->rjkhn", query_all, keys, preferred_element_type=jnp.float32)
        * score_scale
    )
    masked = jnp.where(key_mask, scores, NEG)
    row_peak = jnp.max(masked, axis=-1)
    weights = jnp.where(key_mask, jnp.exp(masked - row_peak[..., None]), 0.0)
    row_total = jnp.sum(weights, axis=-1)
    out = jnp.einsum(
        "rjkhn,nkd->rjkhd", weights.astype(jnp.bfloat16), values, preferred_element_type=jnp.float32
    )

    flat_out = out.reshape(requests, -1)
    stats = jnp.concatenate(
        [row_peak.reshape(requests, -1), row_total.reshape(requests, -1)], axis=1
    )
    packed = jnp.concatenate([flat_out, stats], axis=1)
    received = lax.all_to_all(packed, SEQ, 0, 0, tiled=True)
    received = received.reshape(seq_count, req_dev, -1)
    n_out = flat_out.shape[1]
    n_stat = row_peak.size // requests
    shape_rows = (seq_count, req_dev, NEW, kv_local, HPK)
    part_out = received[:, :, :n_out].reshape(shape_rows + (HEAD_DIM,))
    part_peak = received[:, :, n_out : n_out + n_stat].reshape(shape_rows)
    part_total = received[:, :, n_out + n_stat :].reshape(shape_rows)
    top_peak = jnp.max(part_peak, axis=0)
    factor = jnp.exp(part_peak - top_peak[None])
    final_total = jnp.sum(part_total * factor, axis=0)
    final_out = jnp.sum(part_out * factor[..., None], axis=0)
    row_start = seq_idx * req_dev
    valid_local = lax.dynamic_slice_in_dim(new_valid, row_start, req_dev, 0)
    valid_rows = valid_local.astype(jnp.float32)[:, :, None, None, None]
    attention = (final_out / final_total[..., None] * valid_rows).astype(jnp.bfloat16)
    attention = attention.reshape(req_dev * NEW, heads_local * HEAD_DIM)
    attention = gather_rows(attention)
    terms = jnp.dot(attention, out_weight, preferred_element_type=jnp.float32)
    summed = lax.psum_scatter(terms.astype(jnp.bfloat16), "tp", scatter_dimension=0, tiled=True)
    return summed


def solution(mesh):
    grid = mesh.devices
    n_seq, n_tp = grid.shape
    inner = inner_size(list(grid[:, 0]))
    if inner < 1 or n_seq % inner:
        inner = 1
    mesh = Mesh(grid.reshape(n_seq // inner, inner, n_tp), ("sx", "sz", "tp"))
    placed = (
        P(SEQ, None, "tp"),
        P(SEQ, None, "tp"),
        P(SEQ, None, "tp"),
        P(None, SEQ, "tp"),
        P(None, SEQ, "tp"),
        P(SEQ, None, "tp"),
        P(SEQ, None, "tp"),
        P("tp", SEQ),
        P(),
        P(),
        P(),
        P(SEQ),
        P(SEQ),
        P(),
    )
    return jax.shard_map(
        local, mesh=mesh, in_specs=placed, out_specs=P("tp", SEQ), check_vma=False
    )
```

```python
import jax
import jax.numpy as jnp
from jax import lax
from jax.sharding import Mesh, PartitionSpec as P

HEAD_DIM = 128
HPK = 8
GROUPS = 8
NEW = 4


NEG = -(2.0**100)
SEQ = ("sx", "sz")


def gather_rows(block):
    inner = lax.axis_size("sz")
    copies = jnp.broadcast_to(block[None], (inner,) + block.shape)
    block = lax.all_to_all(copies, "sz", 0, 0, tiled=True)
    block = block.reshape((inner * block.shape[1],) + block.shape[2:])
    return lax.all_gather(block, "sx", axis=0, tiled=True)


def merge(parts, n_out, n_stat):
    part_out = parts[..., :n_out]
    part_peak = parts[..., n_out : n_out + n_stat]
    part_total = parts[..., n_out + n_stat :]
    top_peak = jnp.max(part_peak, axis=0)
    factor = jnp.exp(part_peak - top_peak[None])
    total = jnp.sum(part_total * factor, axis=0)
    lead = factor.shape[:-1]
    rows = factor.reshape(lead + (n_stat, 1))
    out = parts[..., :n_out].reshape(lead + (n_stat, n_out // n_stat)) * rows
    out = jnp.sum(out, axis=0).reshape(out.shape[1:-2] + (n_out,))
    return out, top_peak, total


def inner_size(devices):
    try:
        return len({d.coords[2] for d in devices})
    except Exception:
        return 1


def local(
    queries,
    new_keys,
    new_values,
    prefix_keys,
    prefix_values,
    page_keys,
    page_values,
    out_weight,
    group_of,
    prefix_len,
    total_len,
    page_owner,
    page_slot,
    new_valid,
):
    req_dev = queries.shape[0]
    seq_count = lax.axis_size(SEQ)
    requests = req_dev * seq_count
    kv_local = new_keys.shape[2] // HEAD_DIM
    heads_local = kv_local * HPK
    score_scale = HEAD_DIM ** (-0.5)
    seq_idx = lax.axis_index(SEQ)
    gathered = gather_rows(queries)
    query_all = gathered.reshape(requests, NEW, kv_local, HPK, HEAD_DIM)

    group_hot = group_of[:, None] == jnp.arange(GROUPS, dtype=jnp.int32)[None, :]
    own_prefix = jnp.sum(jnp.where(group_hot, prefix_len[None, :], 0), axis=1)
    suffix_len = total_len - own_prefix

    pre_dev = prefix_keys.shape[1]
    page_count = page_keys.shape[0]
    page_len = page_keys.shape[1]
    keys = jnp.concatenate(
        [
            prefix_keys.reshape(GROUPS * pre_dev, kv_local, HEAD_DIM),
            page_keys.reshape(page_count * page_len, kv_local, HEAD_DIM),
            new_keys.reshape(req_dev * NEW, kv_local, HEAD_DIM),
        ],
        axis=0,
    )
    values = jnp.concatenate(
        [
            prefix_values.reshape(GROUPS * pre_dev, kv_local, HEAD_DIM),
            page_values.reshape(page_count * page_len, kv_local, HEAD_DIM),
            new_values.reshape(req_dev * NEW, kv_local, HEAD_DIM),
        ],
        axis=0,
    )

    req_ids = jnp.arange(requests, dtype=jnp.int32)
    positions = seq_idx * pre_dev + jnp.arange(pre_dev, dtype=jnp.int32)
    pre_live = positions[None, :] < prefix_len[:, None]
    pre_mask = group_hot[:, :, None] & pre_live[None, :, :]
    pre_mask = pre_mask.reshape(requests, 1, GROUPS * pre_dev)
    pre_mask = jnp.broadcast_to(pre_mask, (requests, NEW, GROUPS * pre_dev))
    owner_hot = req_ids[:, None] == page_owner[None, :]
    offsets = page_slot[:, None] * page_len + jnp.arange(page_len, dtype=jnp.int32)[None, :]
    page_live = offsets[None, :, :] < suffix_len[:, None, None]
    page_mask = (owner_hot[:, :, None] & page_live).reshape(requests, 1, page_count * page_len)
    page_mask = jnp.broadcast_to(page_mask, (requests, NEW, page_count * page_len))
    new_owner = seq_idx * req_dev + jnp.arange(req_dev, dtype=jnp.int32)
    tok = jnp.arange(NEW, dtype=jnp.int32)
    causal = tok[None, :] <= tok[:, None]
    new_live = new_valid == 1
    new_mask = (
        (req_ids[:, None, None, None] == new_owner[None, None, :, None])
        & causal[None, :, None, :]
        & new_live[:, None, None, :]
    ).reshape(requests, NEW, req_dev * NEW)
    key_mask = jnp.concatenate([pre_mask, page_mask, new_mask], axis=2)
    key_mask = key_mask[:, :, None, None, :]

    scores = (
        jnp.einsum("rjkhd,nkd->rjkhn", query_all, keys, preferred_element_type=jnp.float32)
        * score_scale
    )
    masked = jnp.where(key_mask, scores, NEG)
    row_peak = jnp.max(masked, axis=-1)
    weights = jnp.where(key_mask, jnp.exp(masked - row_peak[..., None]), 0.0)
    row_total = jnp.sum(weights, axis=-1)
    out = jnp.einsum(
        "rjkhn,nkd->rjkhd", weights.astype(jnp.bfloat16), values, preferred_element_type=jnp.float32
    )

    flat_out = out.reshape(requests, -1)
    peak = row_peak.reshape(requests, -1)
    near_peak = peak.astype(jnp.bfloat16).astype(jnp.float32)
    shift = jnp.exp(peak - near_peak)
    n_stat = peak.shape[1]
    n_out = flat_out.shape[1]
    flat_out = (flat_out.reshape(requests, n_stat, -1) * shift[..., None]).reshape(requests, n_out)
    total = row_total.reshape(requests, -1) * shift
    packed = jnp.concatenate([flat_out, near_peak, total], axis=1).astype(jnp.bfloat16)
    outer = lax.axis_size("sx")
    inner = lax.axis_size("sz")
    width = packed.shape[1]
    packed = packed.reshape(outer, inner, req_dev, width).transpose(1, 0, 2, 3)
    received = lax.all_to_all(packed, "sz", 0, 0, tiled=True).astype(jnp.float32)
    stage_out, stage_peak, stage_total = merge(received, n_out, n_stat)
    packed = jnp.concatenate([stage_out, stage_peak, stage_total], axis=-1)
    received = lax.all_to_all(packed, "sx", 0, 0, tiled=True)
    final_out, _, final_total = merge(received, n_out, n_stat)
    final_out = final_out.reshape(req_dev, NEW, kv_local, HPK, HEAD_DIM)
    final_total = final_total.reshape(req_dev, NEW, kv_local, HPK)
    row_start = seq_idx * req_dev
    valid_local = lax.dynamic_slice_in_dim(new_valid, row_start, req_dev, 0)
    valid_rows = valid_local.astype(jnp.float32)[:, :, None, None, None]
    attention = (final_out / final_total[..., None] * valid_rows).astype(jnp.bfloat16)
    attention = attention.reshape(req_dev * NEW, heads_local * HEAD_DIM)
    attention = gather_rows(attention)
    terms = jnp.dot(attention, out_weight, preferred_element_type=jnp.float32)
    n_tp = lax.axis_size("tp")
    blocks = lax.all_to_all(terms, "tp", 0, 0, tiled=True)
    blocks = blocks.reshape((n_tp, blocks.shape[0] // n_tp) + blocks.shape[1:])
    return jnp.sum(blocks, axis=0).astype(jnp.bfloat16)


def solution(mesh):
    grid = mesh.devices
    n_seq, n_tp = grid.shape
    inner = inner_size(list(grid[:, 0]))
    if inner < 1 or n_seq % inner:
        inner = 1
    mesh = Mesh(grid.reshape(n_seq // inner, inner, n_tp), ("sx", "sz", "tp"))
    placed = (
        P(SEQ, None, "tp"),
        P(SEQ, None, "tp"),
        P(SEQ, None, "tp"),
        P(None, SEQ, "tp"),
        P(None, SEQ, "tp"),
        P(SEQ, None, "tp"),
        P(SEQ, None, "tp"),
        P("tp", SEQ),
        P(),
        P(),
        P(),
        P(SEQ),
        P(SEQ),
        P(),
    )
    return jax.shard_map(
        local, mesh=mesh, in_specs=placed, out_specs=P("tp", SEQ), check_vma=False
    )
```

```python
import jax
import jax.numpy as jnp
from jax import lax
from jax.sharding import Mesh, PartitionSpec as P

HEAD_DIM = 128
HPK = 8
GROUPS = 8
NEW = 4


NEG = -(2.0**100)
SEQ = ("sx", "sz")


def gather_rows(block):
    inner = lax.axis_size("sz")
    copies = jnp.broadcast_to(block[None], (inner,) + block.shape)
    block = lax.all_to_all(copies, "sz", 0, 0, tiled=True)
    block = block.reshape((inner * block.shape[1],) + block.shape[2:])
    return lax.all_gather(block, "sx", axis=0, tiled=True)


def merge(parts, n_out, n_stat):
    part_out = parts[..., :n_out]
    part_peak = parts[..., n_out : n_out + n_stat]
    part_total = parts[..., n_out + n_stat :]
    top_peak = jnp.max(part_peak, axis=0)
    factor = jnp.exp(part_peak - top_peak[None])
    total = jnp.sum(part_total * factor, axis=0)
    lead = factor.shape[:-1]
    rows = factor.reshape(lead + (n_stat, 1))
    out = parts[..., :n_out].reshape(lead + (n_stat, n_out // n_stat)) * rows
    out = jnp.sum(out, axis=0).reshape(out.shape[1:-2] + (n_out,))
    return out, top_peak, total


def inner_size(devices):
    try:
        return len({d.coords[2] for d in devices})
    except Exception:
        return 1


def local(
    queries,
    new_keys,
    new_values,
    prefix_keys,
    prefix_values,
    page_keys,
    page_values,
    out_weight,
    group_of,
    prefix_len,
    total_len,
    page_owner,
    page_slot,
    new_valid,
):
    req_dev = queries.shape[0]
    seq_count = lax.axis_size(SEQ)
    requests = req_dev * seq_count
    kv_local = new_keys.shape[2] // HEAD_DIM
    heads_local = kv_local * HPK
    score_scale = HEAD_DIM ** (-0.5)
    seq_idx = lax.axis_index(SEQ)
    gathered = gather_rows(queries)
    query_all = gathered.reshape(requests, NEW, kv_local, HPK, HEAD_DIM)

    group_hot = group_of[:, None] == jnp.arange(GROUPS, dtype=jnp.int32)[None, :]
    own_prefix = jnp.sum(jnp.where(group_hot, prefix_len[None, :], 0), axis=1)
    suffix_len = total_len - own_prefix

    pre_dev = prefix_keys.shape[1]
    page_count = page_keys.shape[0]
    page_len = page_keys.shape[1]
    keys = jnp.concatenate(
        [
            prefix_keys.reshape(GROUPS * pre_dev, kv_local, HEAD_DIM),
            page_keys.reshape(page_count * page_len, kv_local, HEAD_DIM),
            new_keys.reshape(req_dev * NEW, kv_local, HEAD_DIM),
        ],
        axis=0,
    )
    values = jnp.concatenate(
        [
            prefix_values.reshape(GROUPS * pre_dev, kv_local, HEAD_DIM),
            page_values.reshape(page_count * page_len, kv_local, HEAD_DIM),
            new_values.reshape(req_dev * NEW, kv_local, HEAD_DIM),
        ],
        axis=0,
    )

    req_ids = jnp.arange(requests, dtype=jnp.int32)
    positions = seq_idx * pre_dev + jnp.arange(pre_dev, dtype=jnp.int32)
    pre_live = positions[None, :] < prefix_len[:, None]
    pre_mask = group_hot[:, :, None] & pre_live[None, :, :]
    pre_mask = pre_mask.reshape(requests, 1, GROUPS * pre_dev)
    pre_mask = jnp.broadcast_to(pre_mask, (requests, NEW, GROUPS * pre_dev))
    owner_hot = req_ids[:, None] == page_owner[None, :]
    offsets = page_slot[:, None] * page_len + jnp.arange(page_len, dtype=jnp.int32)[None, :]
    page_live = offsets[None, :, :] < suffix_len[:, None, None]
    page_mask = (owner_hot[:, :, None] & page_live).reshape(requests, 1, page_count * page_len)
    page_mask = jnp.broadcast_to(page_mask, (requests, NEW, page_count * page_len))
    new_owner = seq_idx * req_dev + jnp.arange(req_dev, dtype=jnp.int32)
    tok = jnp.arange(NEW, dtype=jnp.int32)
    causal = tok[None, :] <= tok[:, None]
    new_live = new_valid == 1
    new_mask = (
        (req_ids[:, None, None, None] == new_owner[None, None, :, None])
        & causal[None, :, None, :]
        & new_live[:, None, None, :]
    ).reshape(requests, NEW, req_dev * NEW)
    key_mask = jnp.concatenate([pre_mask, page_mask, new_mask], axis=2)
    key_mask = key_mask[:, :, None, None, :]

    scores = (
        jnp.einsum("rjkhd,nkd->rjkhn", query_all, keys, preferred_element_type=jnp.float32)
        * score_scale
    )
    masked = jnp.where(key_mask, scores, NEG)
    row_peak = jnp.max(masked, axis=-1)
    weights = jnp.where(key_mask, jnp.exp(masked - row_peak[..., None]), 0.0)
    row_total = jnp.sum(weights, axis=-1)
    out = jnp.einsum(
        "rjkhn,nkd->rjkhd", weights.astype(jnp.bfloat16), values, preferred_element_type=jnp.float32
    )

    flat_out = out.reshape(requests, -1)
    peak = row_peak.reshape(requests, -1)
    near_peak = peak.astype(jnp.bfloat16).astype(jnp.float32)
    shift = jnp.exp(peak - near_peak)
    n_stat = peak.shape[1]
    n_out = flat_out.shape[1]
    flat_out = (flat_out.reshape(requests, n_stat, -1) * shift[..., None]).reshape(requests, n_out)
    total = row_total.reshape(requests, -1) * shift
    packed = jnp.concatenate([flat_out, near_peak, total], axis=1).astype(jnp.bfloat16)
    outer = lax.axis_size("sx")
    inner = lax.axis_size("sz")
    width = packed.shape[1]
    packed = packed.reshape(outer, inner, req_dev, width)
    received = lax.all_to_all(packed, "sx", 0, 0, tiled=True).astype(jnp.float32)
    stage_out, stage_peak, stage_total = merge(received, n_out, n_stat)
    packed = jnp.concatenate([stage_out, stage_peak, stage_total], axis=-1)
    received = lax.all_to_all(packed, "sz", 0, 0, tiled=True)
    final_out, _, final_total = merge(received, n_out, n_stat)
    final_out = final_out.reshape(req_dev, NEW, kv_local, HPK, HEAD_DIM)
    final_total = final_total.reshape(req_dev, NEW, kv_local, HPK)
    row_start = seq_idx * req_dev
    valid_local = lax.dynamic_slice_in_dim(new_valid, row_start, req_dev, 0)
    valid_rows = valid_local.astype(jnp.float32)[:, :, None, None, None]
    attention = (final_out / final_total[..., None] * valid_rows).astype(jnp.bfloat16)
    attention = attention.reshape(req_dev * NEW, heads_local * HEAD_DIM)
    attention = gather_rows(attention)
    terms = jnp.dot(attention, out_weight, preferred_element_type=jnp.float32)
    n_tp = lax.axis_size("tp")
    blocks = lax.all_to_all(terms, "tp", 0, 0, tiled=True)
    blocks = blocks.reshape((n_tp, blocks.shape[0] // n_tp) + blocks.shape[1:])
    return jnp.sum(blocks, axis=0).astype(jnp.bfloat16)


def solution(mesh):
    grid = mesh.devices
    n_seq, n_tp = grid.shape
    inner = inner_size(list(grid[:, 0]))
    if inner < 1 or n_seq % inner:
        inner = 1
    mesh = Mesh(grid.reshape(n_seq // inner, inner, n_tp), ("sx", "sz", "tp"))
    placed = (
        P(SEQ, None, "tp"),
        P(SEQ, None, "tp"),
        P(SEQ, None, "tp"),
        P(None, SEQ, "tp"),
        P(None, SEQ, "tp"),
        P(SEQ, None, "tp"),
        P(SEQ, None, "tp"),
        P("tp", SEQ),
        P(),
        P(),
        P(),
        P(SEQ),
        P(SEQ),
        P(),
    )
    return jax.shard_map(
        local, mesh=mesh, in_specs=placed, out_specs=P("tp", SEQ), check_vma=False
    )
```

```python
import jax
import jax.numpy as jnp
from jax import lax
from jax.sharding import Mesh, PartitionSpec as P

HEAD_DIM = 128
HPK = 8
GROUPS = 8
NEW = 4


NEG = -(2.0**100)
SEQ = ("sx", "sz")


def gather_rows(block):
    inner = lax.axis_size("sz")
    copies = jnp.broadcast_to(block[None], (inner,) + block.shape)
    block = lax.all_to_all(copies, "sz", 0, 0, tiled=True)
    block = block.reshape((inner * block.shape[1],) + block.shape[2:])
    return lax.all_gather(block, "sx", axis=0, tiled=True)


def softmax_part(scores, key_mask):
    masked = jnp.where(key_mask, scores, NEG)
    row_peak = jnp.max(masked, axis=-1)
    weights = jnp.where(key_mask, jnp.exp(masked - row_peak[..., None]), 0.0)
    return (row_peak, jnp.sum(weights, axis=-1), weights.astype(jnp.bfloat16))


def merge(parts, n_out, n_stat):
    part_out = parts[..., :n_out]
    part_peak = parts[..., n_out : n_out + n_stat]
    part_total = parts[..., n_out + n_stat :]
    top_peak = jnp.max(part_peak, axis=0)
    factor = jnp.exp(part_peak - top_peak[None])
    total = jnp.sum(part_total * factor, axis=0)
    lead = factor.shape[:-1]
    rows = factor.reshape(lead + (n_stat, 1))
    out = parts[..., :n_out].reshape(lead + (n_stat, n_out // n_stat)) * rows
    out = jnp.sum(out, axis=0).reshape(out.shape[1:-2] + (n_out,))
    return out, top_peak, total


def inner_size(devices):
    try:
        return len({d.coords[2] for d in devices})
    except Exception:
        return 1


def local(
    queries,
    new_keys,
    new_values,
    prefix_keys,
    prefix_values,
    page_keys,
    page_values,
    out_weight,
    group_of,
    prefix_len,
    total_len,
    page_owner,
    page_slot,
    new_valid,
):
    req_dev = queries.shape[0]
    seq_count = lax.axis_size(SEQ)
    requests = req_dev * seq_count
    kv_local = new_keys.shape[2] // HEAD_DIM
    heads_local = kv_local * HPK
    score_scale = HEAD_DIM ** (-0.5)
    seq_idx = lax.axis_index(SEQ)
    gathered = gather_rows(queries)
    query_all = gathered.reshape(requests, NEW, kv_local, HPK, HEAD_DIM)

    group_hot = group_of[:, None] == jnp.arange(GROUPS, dtype=jnp.int32)[None, :]
    own_prefix = jnp.sum(jnp.where(group_hot, prefix_len[None, :], 0), axis=1)
    suffix_len = total_len - own_prefix

    pre_dev = prefix_keys.shape[1]
    page_count = page_keys.shape[0]
    page_len = page_keys.shape[1]
    req_ids = jnp.arange(requests, dtype=jnp.int32)

    pre_k = prefix_keys.reshape(GROUPS, pre_dev, kv_local, HEAD_DIM)
    pre_v = prefix_values.reshape(GROUPS, pre_dev, kv_local, HEAD_DIM)
    req_keys = jnp.take(pre_k, group_of, axis=0)
    req_values = jnp.take(pre_v, group_of, axis=0)
    positions = seq_idx * pre_dev + jnp.arange(pre_dev, dtype=jnp.int32)
    pre_live = positions[None, :] < own_prefix[:, None]
    scores = (
        jnp.einsum("rjkhd,rpkd->rjkhp", query_all, req_keys, preferred_element_type=jnp.float32)
        * score_scale
    )
    pre_peak, pre_total, weights = softmax_part(scores, pre_live[:, None, None, None, :])
    pre_out = jnp.einsum(
        "rjkhp,rpkd->rjkhd", weights, req_values, preferred_element_type=jnp.float32
    )

    page_q = jnp.take(query_all, page_owner, axis=0)
    key_pages = page_keys.reshape(page_count, page_len, kv_local, HEAD_DIM)
    value_pages = page_values.reshape(page_count, page_len, kv_local, HEAD_DIM)
    own_suffix = jnp.take(suffix_len, page_owner)
    offsets = page_slot[:, None] * page_len + jnp.arange(page_len, dtype=jnp.int32)[None, :]
    page_live = offsets < own_suffix[:, None]
    scores = (
        jnp.einsum("qjkhd,qikd->qjkhi", page_q, key_pages, preferred_element_type=jnp.float32)
        * score_scale
    )
    page_peak, page_total, weights = softmax_part(scores, page_live[:, None, None, None, :])
    page_out = jnp.einsum(
        "qjkhi,qikd->qjkhd", weights, value_pages, preferred_element_type=jnp.float32
    )

    row_start = seq_idx * req_dev
    valid_local = lax.dynamic_slice_in_dim(new_valid, row_start, req_dev, 0)
    local_q = queries.reshape(req_dev, NEW, kv_local, HPK, HEAD_DIM)
    local_k = new_keys.reshape(req_dev, NEW, kv_local, HEAD_DIM)
    local_v = new_values.reshape(req_dev, NEW, kv_local, HEAD_DIM)
    tok = jnp.arange(NEW, dtype=jnp.int32)
    causal = tok[None, :] <= tok[:, None]
    new_mask = causal[None, :, None, None, :] & (valid_local[:, None, None, None, :] == 1)
    scores = (
        jnp.einsum("rjkhd,rikd->rjkhi", local_q, local_k, preferred_element_type=jnp.float32)
        * score_scale
    )
    new_peak, new_total, weights = softmax_part(scores, new_mask)
    new_out = jnp.einsum(
        "rjkhi,rikd->rjkhd", weights, local_v, preferred_element_type=jnp.float32
    )

    ex_owner = jnp.concatenate([page_owner, row_start + jnp.arange(req_dev, dtype=jnp.int32)])
    ex_peak = jnp.concatenate([page_peak, new_peak], axis=0)
    ex_total = jnp.concatenate([page_total, new_total], axis=0)
    ex_out = jnp.concatenate([page_out, new_out], axis=0)
    ex_hot = ex_owner[None, :] == req_ids[:, None]
    ex_top = jnp.max(jnp.where(ex_hot[:, :, None, None, None], ex_peak[None], NEG), axis=1)
    row_peak = jnp.maximum(pre_peak, ex_top)
    pre_factor = jnp.exp(pre_peak - row_peak)
    ex_factor = jnp.exp(ex_peak - jnp.take(row_peak, ex_owner, axis=0))
    hot = ex_hot.astype(jnp.float32)
    row_total = pre_total * pre_factor + jnp.einsum(
        "re,ejkh->rjkh", hot, ex_total * ex_factor, precision=lax.Precision.HIGHEST
    )
    out = pre_out * pre_factor[..., None] + jnp.einsum(
        "re,ejkhd->rjkhd", hot, ex_out * ex_factor[..., None], precision=lax.Precision.HIGHEST
    )

    flat_out = out.reshape(requests, -1)
    peak = row_peak.reshape(requests, -1)
    near_peak = peak.astype(jnp.bfloat16).astype(jnp.float32)
    shift = jnp.exp(peak - near_peak)
    n_stat = peak.shape[1]
    n_out = flat_out.shape[1]
    flat_out = (flat_out.reshape(requests, n_stat, -1) * shift[..., None]).reshape(requests, n_out)
    total = row_total.reshape(requests, -1) * shift
    packed = jnp.concatenate([flat_out, near_peak, total], axis=1).astype(jnp.bfloat16)
    outer = lax.axis_size("sx")
    inner = lax.axis_size("sz")
    width = packed.shape[1]
    packed = packed.reshape(outer, inner, req_dev, width)
    received = lax.all_to_all(packed, "sx", 0, 0, tiled=True).astype(jnp.float32)
    stage_out, stage_peak, stage_total = merge(received, n_out, n_stat)
    packed = jnp.concatenate([stage_out, stage_peak, stage_total], axis=-1)
    received = lax.all_to_all(packed, "sz", 0, 0, tiled=True)
    final_out, _, final_total = merge(received, n_out, n_stat)
    final_out = final_out.reshape(req_dev, NEW, kv_local, HPK, HEAD_DIM)
    final_total = final_total.reshape(req_dev, NEW, kv_local, HPK)
    valid_rows = valid_local.astype(jnp.float32)[:, :, None, None, None]
    attention = (final_out / final_total[..., None] * valid_rows).astype(jnp.bfloat16)
    attention = attention.reshape(req_dev * NEW, heads_local * HEAD_DIM)
    attention = gather_rows(attention)
    terms = jnp.dot(attention, out_weight, preferred_element_type=jnp.float32)
    n_tp = lax.axis_size("tp")
    blocks = lax.all_to_all(terms, "tp", 0, 0, tiled=True)
    blocks = blocks.reshape((n_tp, blocks.shape[0] // n_tp) + blocks.shape[1:])
    return jnp.sum(blocks, axis=0).astype(jnp.bfloat16)


def solution(mesh):
    grid = mesh.devices
    n_seq, n_tp = grid.shape
    inner = inner_size(list(grid[:, 0]))
    if inner < 1 or n_seq % inner:
        inner = 1
    mesh = Mesh(grid.reshape(n_seq // inner, inner, n_tp), ("sx", "sz", "tp"))
    placed = (
        P(SEQ, None, "tp"),
        P(SEQ, None, "tp"),
        P(SEQ, None, "tp"),
        P(None, SEQ, "tp"),
        P(None, SEQ, "tp"),
        P(SEQ, None, "tp"),
        P(SEQ, None, "tp"),
        P("tp", SEQ),
        P(),
        P(),
        P(),
        P(SEQ),
        P(SEQ),
        P(),
    )
    return jax.shard_map(
        local, mesh=mesh, in_specs=placed, out_specs=P("tp", SEQ), check_vma=False
    )
```

```python
import functools

import jax
import jax.numpy as jnp
from jax import lax
from jax.experimental import pallas as pl
from jax.experimental.pallas import tpu as pltpu
from jax.sharding import Mesh, PartitionSpec as P

HEAD_DIM = 128
HPK = 8
GROUPS = 8
NEW = 4


NEG = -(2.0**100)
SEQ = ("sx", "sz")


def gather_rows(block):
    inner = lax.axis_size("sz")
    copies = jnp.broadcast_to(block[None], (inner,) + block.shape)
    block = lax.all_to_all(copies, "sz", 0, 0, tiled=True)
    block = block.reshape((inner * block.shape[1],) + block.shape[2:])
    return lax.all_gather(block, "sx", axis=0, tiled=True)


def attend_kernel(scale, q_ref, k_ref, v_ref, keep_ref, o_ref, m_ref, l_ref):
    scores = lax.dot_general(
        q_ref[...], k_ref[0], (((1,), (1,)), ((), ())), preferred_element_type=jnp.float32
    )
    scores = scores * scale
    keep = keep_ref[...] > 0.5
    masked = jnp.where(keep, scores, NEG)
    peak = jnp.max(masked, axis=1, keepdims=True)
    weights = jnp.where(keep, jnp.exp(masked - peak), 0.0)
    total = jnp.sum(weights, axis=1, keepdims=True)
    o_ref[...] = jnp.dot(
        weights.astype(jnp.bfloat16), v_ref[0], preferred_element_type=jnp.float32
    )
    m_ref[...] = jnp.broadcast_to(peak, m_ref.shape)
    l_ref[...] = jnp.broadcast_to(total, l_ref.shape)


def attend(query_all, keys, values, key_mask, scale):
    requests, new, kv, hpk, dim = query_all.shape
    n_keys = keys.shape[0]
    padded = -(-n_keys // 128) * 128
    rows = requests * new
    pad = ((0, padded - n_keys), (0, 0), (0, 0))
    keys_t = jnp.pad(keys, pad).transpose(1, 0, 2)
    values_t = jnp.pad(values, pad).transpose(1, 0, 2)
    keep = jnp.pad(key_mask, ((0, 0), (0, 0), (0, padded - n_keys)))
    keep = keep.reshape(rows, padded).astype(jnp.float32)
    q_rows = query_all.transpose(2, 3, 0, 1, 4).reshape(kv * hpk * rows, dim)
    row_block = pl.BlockSpec((rows, dim), lambda i: (i, 0))
    kv_block = pl.BlockSpec((1, padded, dim), lambda i: (i // hpk, 0, 0))
    stat = jax.ShapeDtypeStruct((kv * hpk * rows, dim), jnp.float32)
    out, peak, total = pl.pallas_call(
        functools.partial(attend_kernel, scale),
        grid=(kv * hpk,),
        in_specs=[row_block, kv_block, kv_block, pl.BlockSpec((rows, padded), lambda i: (0, 0))],
        out_specs=[row_block, row_block, row_block],
        out_shape=[stat, stat, stat],
        compiler_params=pltpu.CompilerParams(vmem_limit_bytes=48 * 1024 * 1024),
    )(q_rows, keys_t, values_t, keep)
    out = out.reshape(kv, hpk, requests, new, dim).transpose(2, 3, 0, 1, 4)
    peak = peak[:, 0].reshape(kv, hpk, requests, new).transpose(2, 3, 0, 1)
    total = total[:, 0].reshape(kv, hpk, requests, new).transpose(2, 3, 0, 1)
    return out, peak, total


def merge(parts, n_out, n_stat):
    part_out = parts[..., :n_out]
    part_peak = parts[..., n_out : n_out + n_stat]
    part_total = parts[..., n_out + n_stat :]
    top_peak = jnp.max(part_peak, axis=0)
    factor = jnp.exp(part_peak - top_peak[None])
    total = jnp.sum(part_total * factor, axis=0)
    lead = factor.shape[:-1]
    rows = factor.reshape(lead + (n_stat, 1))
    out = parts[..., :n_out].reshape(lead + (n_stat, n_out // n_stat)) * rows
    out = jnp.sum(out, axis=0).reshape(out.shape[1:-2] + (n_out,))
    return out, top_peak, total


def inner_size(devices):
    try:
        return len({d.coords[2] for d in devices})
    except Exception:
        return 1


def local(
    queries,
    new_keys,
    new_values,
    prefix_keys,
    prefix_values,
    page_keys,
    page_values,
    out_weight,
    group_of,
    prefix_len,
    total_len,
    page_owner,
    page_slot,
    new_valid,
):
    req_dev = queries.shape[0]
    seq_count = lax.axis_size(SEQ)
    requests = req_dev * seq_count
    kv_local = new_keys.shape[2] // HEAD_DIM
    heads_local = kv_local * HPK
    score_scale = HEAD_DIM ** (-0.5)
    seq_idx = lax.axis_index(SEQ)
    gathered = gather_rows(queries)
    query_all = gathered.reshape(requests, NEW, kv_local, HPK, HEAD_DIM)

    group_hot = group_of[:, None] == jnp.arange(GROUPS, dtype=jnp.int32)[None, :]
    own_prefix = jnp.sum(jnp.where(group_hot, prefix_len[None, :], 0), axis=1)
    suffix_len = total_len - own_prefix

    pre_dev = prefix_keys.shape[1]
    page_count = page_keys.shape[0]
    page_len = page_keys.shape[1]
    keys = jnp.concatenate(
        [
            prefix_keys.reshape(GROUPS * pre_dev, kv_local, HEAD_DIM),
            page_keys.reshape(page_count * page_len, kv_local, HEAD_DIM),
            new_keys.reshape(req_dev * NEW, kv_local, HEAD_DIM),
        ],
        axis=0,
    )
    values = jnp.concatenate(
        [
            prefix_values.reshape(GROUPS * pre_dev, kv_local, HEAD_DIM),
            page_values.reshape(page_count * page_len, kv_local, HEAD_DIM),
            new_values.reshape(req_dev * NEW, kv_local, HEAD_DIM),
        ],
        axis=0,
    )

    req_ids = jnp.arange(requests, dtype=jnp.int32)
    positions = seq_idx * pre_dev + jnp.arange(pre_dev, dtype=jnp.int32)
    pre_live = positions[None, :] < prefix_len[:, None]
    pre_mask = group_hot[:, :, None] & pre_live[None, :, :]
    pre_mask = pre_mask.reshape(requests, 1, GROUPS * pre_dev)
    pre_mask = jnp.broadcast_to(pre_mask, (requests, NEW, GROUPS * pre_dev))
    owner_hot = req_ids[:, None] == page_owner[None, :]
    offsets = page_slot[:, None] * page_len + jnp.arange(page_len, dtype=jnp.int32)[None, :]
    page_live = offsets[None, :, :] < suffix_len[:, None, None]
    page_mask = (owner_hot[:, :, None] & page_live).reshape(requests, 1, page_count * page_len)
    page_mask = jnp.broadcast_to(page_mask, (requests, NEW, page_count * page_len))
    new_owner = seq_idx * req_dev + jnp.arange(req_dev, dtype=jnp.int32)
    tok = jnp.arange(NEW, dtype=jnp.int32)
    causal = tok[None, :] <= tok[:, None]
    new_live = new_valid == 1
    new_mask = (
        (req_ids[:, None, None, None] == new_owner[None, None, :, None])
        & causal[None, :, None, :]
        & new_live[:, None, None, :]
    ).reshape(requests, NEW, req_dev * NEW)
    key_mask = jnp.concatenate([pre_mask, page_mask, new_mask], axis=2)
    out, row_peak, row_total = attend(query_all, keys, values, key_mask, score_scale)

    flat_out = out.reshape(requests, -1)
    peak = row_peak.reshape(requests, -1)
    near_peak = peak.astype(jnp.bfloat16).astype(jnp.float32)
    shift = jnp.exp(peak - near_peak)
    n_stat = peak.shape[1]
    n_out = flat_out.shape[1]
    flat_out = (flat_out.reshape(requests, n_stat, -1) * shift[..., None]).reshape(requests, n_out)
    total = row_total.reshape(requests, -1) * shift
    packed = jnp.concatenate([flat_out, near_peak, total], axis=1).astype(jnp.bfloat16)
    outer = lax.axis_size("sx")
    inner = lax.axis_size("sz")
    width = packed.shape[1]
    packed = packed.reshape(outer, inner, req_dev, width)
    received = lax.all_to_all(packed, "sx", 0, 0, tiled=True).astype(jnp.float32)
    stage_out, stage_peak, stage_total = merge(received, n_out, n_stat)
    packed = jnp.concatenate([stage_out, stage_peak, stage_total], axis=-1)
    received = lax.all_to_all(packed, "sz", 0, 0, tiled=True)
    final_out, _, final_total = merge(received, n_out, n_stat)
    final_out = final_out.reshape(req_dev, NEW, kv_local, HPK, HEAD_DIM)
    final_total = final_total.reshape(req_dev, NEW, kv_local, HPK)
    row_start = seq_idx * req_dev
    valid_local = lax.dynamic_slice_in_dim(new_valid, row_start, req_dev, 0)
    valid_rows = valid_local.astype(jnp.float32)[:, :, None, None, None]
    attention = (final_out / final_total[..., None] * valid_rows).astype(jnp.bfloat16)
    attention = attention.reshape(req_dev * NEW, heads_local * HEAD_DIM)
    attention = gather_rows(attention)
    terms = jnp.dot(attention, out_weight, preferred_element_type=jnp.float32)
    n_tp = lax.axis_size("tp")
    blocks = lax.all_to_all(terms, "tp", 0, 0, tiled=True)
    blocks = blocks.reshape((n_tp, blocks.shape[0] // n_tp) + blocks.shape[1:])
    return jnp.sum(blocks, axis=0).astype(jnp.bfloat16)


def solution(mesh):
    grid = mesh.devices
    n_seq, n_tp = grid.shape
    inner = inner_size(list(grid[:, 0]))
    if inner < 1 or n_seq % inner:
        inner = 1
    mesh = Mesh(grid.reshape(n_seq // inner, inner, n_tp), ("sx", "sz", "tp"))
    placed = (
        P(SEQ, None, "tp"),
        P(SEQ, None, "tp"),
        P(SEQ, None, "tp"),
        P(None, SEQ, "tp"),
        P(None, SEQ, "tp"),
        P(SEQ, None, "tp"),
        P(SEQ, None, "tp"),
        P("tp", SEQ),
        P(),
        P(),
        P(),
        P(SEQ),
        P(SEQ),
        P(),
    )
    return jax.shard_map(
        local, mesh=mesh, in_specs=placed, out_specs=P("tp", SEQ), check_vma=False
    )
```

```python
import functools

import jax
import jax.numpy as jnp
from jax import lax
from jax.experimental import pallas as pl
from jax.experimental.pallas import tpu as pltpu
from jax.sharding import Mesh, PartitionSpec as P

HEAD_DIM = 128
HPK = 8
GROUPS = 8
NEW = 4


NEG = -(2.0**100)
SEQ = ("sx", "sz")


def gather_rows(block):
    inner = lax.axis_size("sz")
    copies = jnp.broadcast_to(block[None], (inner,) + block.shape)
    block = lax.all_to_all(copies, "sz", 0, 0, tiled=True)
    block = block.reshape((inner * block.shape[1],) + block.shape[2:])
    return lax.all_gather(block, "sx", axis=0, tiled=True)


def attend_kernel(scale, q_ref, k_ref, v_ref, keep_ref, o_ref, m_ref, l_ref):
    scores = lax.dot_general(
        q_ref[...], k_ref[0], (((1,), (1,)), ((), ())), preferred_element_type=jnp.float32
    )
    scores = scores * scale
    keep = keep_ref[...] > 0.5
    masked = jnp.where(keep, scores, NEG)
    peak = jnp.max(masked, axis=1, keepdims=True)
    weights = jnp.exp(masked - jnp.maximum(peak, 0.5 * NEG))
    total = jnp.sum(weights, axis=1, keepdims=True)
    o_ref[...] = jnp.dot(
        weights.astype(jnp.bfloat16), v_ref[0], preferred_element_type=jnp.float32
    )
    m_ref[...] = jnp.broadcast_to(peak, m_ref.shape)
    l_ref[...] = jnp.broadcast_to(total, l_ref.shape)


def attend(query_all, keys, values, key_mask, scale):
    requests, new, kv, hpk, dim = query_all.shape
    n_keys = keys.shape[0]
    padded = -(-n_keys // 128) * 128
    rows = requests * new
    pad = ((0, padded - n_keys), (0, 0), (0, 0))
    keys_t = jnp.pad(keys, pad).transpose(1, 0, 2)
    values_t = jnp.pad(values, pad).transpose(1, 0, 2)
    keep = jnp.pad(key_mask, ((0, 0), (0, 0), (0, padded - n_keys)))
    keep = keep.reshape(rows, padded).astype(jnp.bfloat16)
    q_rows = query_all.transpose(2, 3, 0, 1, 4).reshape(kv * hpk * rows, dim)
    row_block = pl.BlockSpec((rows, dim), lambda i: (i, 0))
    kv_block = pl.BlockSpec((1, padded, dim), lambda i: (i // hpk, 0, 0))
    stat = jax.ShapeDtypeStruct((kv * hpk * rows, dim), jnp.float32)
    out, peak, total = pl.pallas_call(
        functools.partial(attend_kernel, scale),
        grid=(kv * hpk,),
        in_specs=[row_block, kv_block, kv_block, pl.BlockSpec((rows, padded), lambda i: (0, 0))],
        out_specs=[row_block, row_block, row_block],
        out_shape=[stat, stat, stat],
        compiler_params=pltpu.CompilerParams(vmem_limit_bytes=48 * 1024 * 1024),
    )(q_rows, keys_t, values_t, keep)
    out = out.reshape(kv, hpk, requests, new, dim).transpose(2, 3, 0, 1, 4)
    peak = peak[:, 0].reshape(kv, hpk, requests, new).transpose(2, 3, 0, 1)
    total = total[:, 0].reshape(kv, hpk, requests, new).transpose(2, 3, 0, 1)
    return out, peak, total


def merge(parts, n_out, n_stat):
    part_out = parts[..., :n_out]
    part_peak = parts[..., n_out : n_out + n_stat]
    part_total = parts[..., n_out + n_stat :]
    top_peak = jnp.max(part_peak, axis=0)
    factor = jnp.exp(part_peak - top_peak[None])
    total = jnp.sum(part_total * factor, axis=0)
    lead = factor.shape[:-1]
    rows = factor.reshape(lead + (n_stat, 1))
    out = parts[..., :n_out].reshape(lead + (n_stat, n_out // n_stat)) * rows
    out = jnp.sum(out, axis=0).reshape(out.shape[1:-2] + (n_out,))
    return out, top_peak, total


def inner_size(devices):
    try:
        return len({d.coords[2] for d in devices})
    except Exception:
        return 1


def local(
    queries,
    new_keys,
    new_values,
    prefix_keys,
    prefix_values,
    page_keys,
    page_values,
    out_weight,
    group_of,
    prefix_len,
    total_len,
    page_owner,
    page_slot,
    new_valid,
):
    req_dev = queries.shape[0]
    seq_count = lax.axis_size(SEQ)
    requests = req_dev * seq_count
    kv_local = new_keys.shape[2] // HEAD_DIM
    heads_local = kv_local * HPK
    score_scale = HEAD_DIM ** (-0.5)
    seq_idx = lax.axis_index(SEQ)
    gathered = gather_rows(queries)
    query_all = gathered.reshape(requests, NEW, kv_local, HPK, HEAD_DIM)

    group_hot = group_of[:, None] == jnp.arange(GROUPS, dtype=jnp.int32)[None, :]
    own_prefix = jnp.sum(jnp.where(group_hot, prefix_len[None, :], 0), axis=1)
    suffix_len = total_len - own_prefix

    pre_dev = prefix_keys.shape[1]
    page_count = page_keys.shape[0]
    page_len = page_keys.shape[1]
    keys = jnp.concatenate(
        [
            prefix_keys.reshape(GROUPS * pre_dev, kv_local, HEAD_DIM),
            page_keys.reshape(page_count * page_len, kv_local, HEAD_DIM),
            new_keys.reshape(req_dev * NEW, kv_local, HEAD_DIM),
        ],
        axis=0,
    )
    values = jnp.concatenate(
        [
            prefix_values.reshape(GROUPS * pre_dev, kv_local, HEAD_DIM),
            page_values.reshape(page_count * page_len, kv_local, HEAD_DIM),
            new_values.reshape(req_dev * NEW, kv_local, HEAD_DIM),
        ],
        axis=0,
    )

    req_ids = jnp.arange(requests, dtype=jnp.int32)
    positions = seq_idx * pre_dev + jnp.arange(pre_dev, dtype=jnp.int32)
    pre_live = positions[None, :] < prefix_len[:, None]
    pre_mask = group_hot[:, :, None] & pre_live[None, :, :]
    pre_mask = pre_mask.reshape(requests, 1, GROUPS * pre_dev)
    pre_mask = jnp.broadcast_to(pre_mask, (requests, NEW, GROUPS * pre_dev))
    owner_hot = req_ids[:, None] == page_owner[None, :]
    offsets = page_slot[:, None] * page_len + jnp.arange(page_len, dtype=jnp.int32)[None, :]
    page_live = offsets[None, :, :] < suffix_len[:, None, None]
    page_mask = (owner_hot[:, :, None] & page_live).reshape(requests, 1, page_count * page_len)
    page_mask = jnp.broadcast_to(page_mask, (requests, NEW, page_count * page_len))
    new_owner = seq_idx * req_dev + jnp.arange(req_dev, dtype=jnp.int32)
    tok = jnp.arange(NEW, dtype=jnp.int32)
    causal = tok[None, :] <= tok[:, None]
    new_live = new_valid == 1
    new_mask = (
        (req_ids[:, None, None, None] == new_owner[None, None, :, None])
        & causal[None, :, None, :]
        & new_live[:, None, None, :]
    ).reshape(requests, NEW, req_dev * NEW)
    key_mask = jnp.concatenate([pre_mask, page_mask, new_mask], axis=2)
    out, row_peak, row_total = attend(query_all, keys, values, key_mask, score_scale)

    flat_out = out.reshape(requests, -1)
    peak = row_peak.reshape(requests, -1)
    near_peak = peak.astype(jnp.bfloat16).astype(jnp.float32)
    shift = jnp.exp(peak - near_peak)
    n_stat = peak.shape[1]
    n_out = flat_out.shape[1]
    flat_out = (flat_out.reshape(requests, n_stat, -1) * shift[..., None]).reshape(requests, n_out)
    total = row_total.reshape(requests, -1) * shift
    packed = jnp.concatenate([flat_out, near_peak, total], axis=1).astype(jnp.bfloat16)
    outer = lax.axis_size("sx")
    inner = lax.axis_size("sz")
    width = packed.shape[1]
    packed = packed.reshape(outer, inner, req_dev, width)
    received = lax.all_to_all(packed, "sx", 0, 0, tiled=True).astype(jnp.float32)
    stage_out, stage_peak, stage_total = merge(received, n_out, n_stat)
    packed = jnp.concatenate([stage_out, stage_peak, stage_total], axis=-1)
    received = lax.all_to_all(packed, "sz", 0, 0, tiled=True)
    final_out, _, final_total = merge(received, n_out, n_stat)
    final_out = final_out.reshape(req_dev, NEW, kv_local, HPK, HEAD_DIM)
    final_total = final_total.reshape(req_dev, NEW, kv_local, HPK)
    row_start = seq_idx * req_dev
    valid_local = lax.dynamic_slice_in_dim(new_valid, row_start, req_dev, 0)
    valid_rows = valid_local.astype(jnp.float32)[:, :, None, None, None]
    attention = (final_out / final_total[..., None] * valid_rows).astype(jnp.bfloat16)
    attention = attention.reshape(req_dev * NEW, heads_local * HEAD_DIM)
    attention = gather_rows(attention)
    terms = jnp.dot(attention, out_weight, preferred_element_type=jnp.float32)
    n_tp = lax.axis_size("tp")
    blocks = lax.all_to_all(terms, "tp", 0, 0, tiled=True)
    blocks = blocks.reshape((n_tp, blocks.shape[0] // n_tp) + blocks.shape[1:])
    return jnp.sum(blocks, axis=0).astype(jnp.bfloat16)


def solution(mesh):
    grid = mesh.devices
    n_seq, n_tp = grid.shape
    inner = inner_size(list(grid[:, 0]))
    if inner < 1 or n_seq % inner:
        inner = 1
    mesh = Mesh(grid.reshape(n_seq // inner, inner, n_tp), ("sx", "sz", "tp"))
    placed = (
        P(SEQ, None, "tp"),
        P(SEQ, None, "tp"),
        P(SEQ, None, "tp"),
        P(None, SEQ, "tp"),
        P(None, SEQ, "tp"),
        P(SEQ, None, "tp"),
        P(SEQ, None, "tp"),
        P("tp", SEQ),
        P(),
        P(),
        P(),
        P(SEQ),
        P(SEQ),
        P(),
    )
    return jax.shard_map(
        local, mesh=mesh, in_specs=placed, out_specs=P("tp", SEQ), check_vma=False
    )
```

```python
import functools

import jax
import jax.numpy as jnp
from jax import lax
from jax.experimental import pallas as pl
from jax.experimental.pallas import tpu as pltpu
from jax.sharding import Mesh, PartitionSpec as P

HEAD_DIM = 128
HPK = 8
GROUPS = 8
NEW = 4


NEG = -(2.0**100)
SEQ = ("sx", "sz")


def gather_rows(block):
    inner = lax.axis_size("sz")
    copies = jnp.broadcast_to(block[None], (inner,) + block.shape)
    block = lax.all_to_all(copies, "sz", 0, 0, tiled=True)
    block = block.reshape((inner * block.shape[1],) + block.shape[2:])
    return lax.all_gather(block, "sx", axis=0, tiled=True)


def attend_kernel(scale, q_ref, k_ref, v_ref, keep_ref, o_ref, m_ref, l_ref):
    scores = lax.dot_general(
        q_ref[...], k_ref[0], (((1,), (1,)), ((), ())), preferred_element_type=jnp.float32
    )
    scores = scores * scale
    keep = keep_ref[...] > 0.5
    masked = jnp.where(keep, scores, NEG)
    peak = jnp.max(masked, axis=1, keepdims=True)
    weights = jnp.exp(masked - jnp.maximum(peak, 0.5 * NEG))
    total = jnp.sum(weights, axis=1, keepdims=True)
    o_ref[...] = jnp.dot(
        weights.astype(jnp.bfloat16), v_ref[0], preferred_element_type=jnp.float32
    )
    m_ref[...] = jnp.broadcast_to(peak, m_ref.shape)
    l_ref[...] = jnp.broadcast_to(total, l_ref.shape)


def attend(query_all, keys, values, key_mask, scale):
    requests, new, kv, hpk, dim = query_all.shape
    n_keys = keys.shape[0]
    padded = -(-n_keys // 128) * 128
    rows = requests * new * hpk
    block = 256 if rows % 256 == 0 else rows
    steps = rows // block
    pad = ((0, padded - n_keys), (0, 0), (0, 0))
    keys_t = jnp.pad(keys, pad).transpose(1, 0, 2)
    values_t = jnp.pad(values, pad).transpose(1, 0, 2)
    keep = jnp.pad(key_mask, ((0, 0), (0, 0), (0, padded - n_keys))).astype(jnp.bfloat16)
    keep = jnp.broadcast_to(keep[:, :, None, :], (requests, new, hpk, padded))
    keep = keep.reshape(rows, padded)
    q_rows = query_all.transpose(2, 0, 1, 3, 4).reshape(kv * rows, dim)
    row_block = pl.BlockSpec((block, dim), lambda i: (i, 0))
    kv_block = pl.BlockSpec((1, padded, dim), lambda i: (i // steps, 0, 0))
    keep_block = pl.BlockSpec((block, padded), lambda i: (i % steps, 0))
    stat = jax.ShapeDtypeStruct((kv * rows, dim), jnp.float32)
    out, peak, total = pl.pallas_call(
        functools.partial(attend_kernel, scale),
        grid=(kv * steps,),
        in_specs=[row_block, kv_block, kv_block, keep_block],
        out_specs=[row_block, row_block, row_block],
        out_shape=[stat, stat, stat],
        compiler_params=pltpu.CompilerParams(vmem_limit_bytes=48 * 1024 * 1024),
    )(q_rows, keys_t, values_t, keep)
    out = out.reshape(kv, requests, new, hpk, dim).transpose(1, 2, 0, 3, 4)
    peak = peak[:, 0].reshape(kv, requests, new, hpk).transpose(1, 2, 0, 3)
    total = total[:, 0].reshape(kv, requests, new, hpk).transpose(1, 2, 0, 3)
    return out, peak, total


def merge(parts, n_out, n_stat):
    part_out = parts[..., :n_out]
    part_peak = parts[..., n_out : n_out + n_stat]
    part_total = parts[..., n_out + n_stat :]
    top_peak = jnp.max(part_peak, axis=0)
    factor = jnp.exp(part_peak - top_peak[None])
    total = jnp.sum(part_total * factor, axis=0)
    lead = factor.shape[:-1]
    rows = factor.reshape(lead + (n_stat, 1))
    out = parts[..., :n_out].reshape(lead + (n_stat, n_out // n_stat)) * rows
    out = jnp.sum(out, axis=0).reshape(out.shape[1:-2] + (n_out,))
    return out, top_peak, total


def inner_size(devices):
    try:
        return len({d.coords[2] for d in devices})
    except Exception:
        return 1


def local(
    queries,
    new_keys,
    new_values,
    prefix_keys,
    prefix_values,
    page_keys,
    page_values,
    out_weight,
    group_of,
    prefix_len,
    total_len,
    page_owner,
    page_slot,
    new_valid,
):
    req_dev = queries.shape[0]
    seq_count = lax.axis_size(SEQ)
    requests = req_dev * seq_count
    kv_local = new_keys.shape[2] // HEAD_DIM
    heads_local = kv_local * HPK
    score_scale = HEAD_DIM ** (-0.5)
    seq_idx = lax.axis_index(SEQ)
    gathered = gather_rows(queries)
    query_all = gathered.reshape(requests, NEW, kv_local, HPK, HEAD_DIM)

    group_hot = group_of[:, None] == jnp.arange(GROUPS, dtype=jnp.int32)[None, :]
    own_prefix = jnp.sum(jnp.where(group_hot, prefix_len[None, :], 0), axis=1)
    suffix_len = total_len - own_prefix

    pre_dev = prefix_keys.shape[1]
    page_count = page_keys.shape[0]
    page_len = page_keys.shape[1]
    keys = jnp.concatenate(
        [
            prefix_keys.reshape(GROUPS * pre_dev, kv_local, HEAD_DIM),
            page_keys.reshape(page_count * page_len, kv_local, HEAD_DIM),
            new_keys.reshape(req_dev * NEW, kv_local, HEAD_DIM),
        ],
        axis=0,
    )
    values = jnp.concatenate(
        [
            prefix_values.reshape(GROUPS * pre_dev, kv_local, HEAD_DIM),
            page_values.reshape(page_count * page_len, kv_local, HEAD_DIM),
            new_values.reshape(req_dev * NEW, kv_local, HEAD_DIM),
        ],
        axis=0,
    )

    req_ids = jnp.arange(requests, dtype=jnp.int32)
    positions = seq_idx * pre_dev + jnp.arange(pre_dev, dtype=jnp.int32)
    pre_live = positions[None, :] < prefix_len[:, None]
    pre_mask = group_hot[:, :, None] & pre_live[None, :, :]
    pre_mask = pre_mask.reshape(requests, 1, GROUPS * pre_dev)
    pre_mask = jnp.broadcast_to(pre_mask, (requests, NEW, GROUPS * pre_dev))
    owner_hot = req_ids[:, None] == page_owner[None, :]
    offsets = page_slot[:, None] * page_len + jnp.arange(page_len, dtype=jnp.int32)[None, :]
    page_live = offsets[None, :, :] < suffix_len[:, None, None]
    page_mask = (owner_hot[:, :, None] & page_live).reshape(requests, 1, page_count * page_len)
    page_mask = jnp.broadcast_to(page_mask, (requests, NEW, page_count * page_len))
    new_owner = seq_idx * req_dev + jnp.arange(req_dev, dtype=jnp.int32)
    tok = jnp.arange(NEW, dtype=jnp.int32)
    causal = tok[None, :] <= tok[:, None]
    new_live = new_valid == 1
    new_mask = (
        (req_ids[:, None, None, None] == new_owner[None, None, :, None])
        & causal[None, :, None, :]
        & new_live[:, None, None, :]
    ).reshape(requests, NEW, req_dev * NEW)
    key_mask = jnp.concatenate([pre_mask, page_mask, new_mask], axis=2)
    out, row_peak, row_total = attend(query_all, keys, values, key_mask, score_scale)

    flat_out = out.reshape(requests, -1)
    peak = row_peak.reshape(requests, -1)
    near_peak = peak.astype(jnp.bfloat16).astype(jnp.float32)
    shift = jnp.exp(peak - near_peak)
    n_stat = peak.shape[1]
    n_out = flat_out.shape[1]
    flat_out = (flat_out.reshape(requests, n_stat, -1) * shift[..., None]).reshape(requests, n_out)
    total = row_total.reshape(requests, -1) * shift
    packed = jnp.concatenate([flat_out, near_peak, total], axis=1).astype(jnp.bfloat16)
    outer = lax.axis_size("sx")
    inner = lax.axis_size("sz")
    width = packed.shape[1]
    packed = packed.reshape(outer, inner, req_dev, width)
    received = lax.all_to_all(packed, "sx", 0, 0, tiled=True).astype(jnp.float32)
    stage_out, stage_peak, stage_total = merge(received, n_out, n_stat)
    packed = jnp.concatenate([stage_out, stage_peak, stage_total], axis=-1)
    received = lax.all_to_all(packed, "sz", 0, 0, tiled=True)
    final_out, _, final_total = merge(received, n_out, n_stat)
    final_out = final_out.reshape(req_dev, NEW, kv_local, HPK, HEAD_DIM)
    final_total = final_total.reshape(req_dev, NEW, kv_local, HPK)
    row_start = seq_idx * req_dev
    valid_local = lax.dynamic_slice_in_dim(new_valid, row_start, req_dev, 0)
    valid_rows = valid_local.astype(jnp.float32)[:, :, None, None, None]
    attention = (final_out / final_total[..., None] * valid_rows).astype(jnp.bfloat16)
    attention = attention.reshape(req_dev * NEW, heads_local * HEAD_DIM)
    attention = gather_rows(attention)
    terms = jnp.dot(attention, out_weight, preferred_element_type=jnp.float32)
    n_tp = lax.axis_size("tp")
    blocks = lax.all_to_all(terms, "tp", 0, 0, tiled=True)
    blocks = blocks.reshape((n_tp, blocks.shape[0] // n_tp) + blocks.shape[1:])
    return jnp.sum(blocks, axis=0).astype(jnp.bfloat16)


def solution(mesh):
    grid = mesh.devices
    n_seq, n_tp = grid.shape
    inner = inner_size(list(grid[:, 0]))
    if inner < 1 or n_seq % inner:
        inner = 1
    mesh = Mesh(grid.reshape(n_seq // inner, inner, n_tp), ("sx", "sz", "tp"))
    placed = (
        P(SEQ, None, "tp"),
        P(SEQ, None, "tp"),
        P(SEQ, None, "tp"),
        P(None, SEQ, "tp"),
        P(None, SEQ, "tp"),
        P(SEQ, None, "tp"),
        P(SEQ, None, "tp"),
        P("tp", SEQ),
        P(),
        P(),
        P(),
        P(SEQ),
        P(SEQ),
        P(),
    )
    return jax.shard_map(
        local, mesh=mesh, in_specs=placed, out_specs=P("tp", SEQ), check_vma=False
    )
```

```python
import functools

import jax
import jax.numpy as jnp
from jax import lax
from jax.experimental import pallas as pl
from jax.experimental.pallas import tpu as pltpu
from jax.sharding import Mesh, PartitionSpec as P

HEAD_DIM = 128
HPK = 8
GROUPS = 8
NEW = 4


NEG = -(2.0**100)
SEQ = ("sx", "sz")


def gather_rows(block):
    inner = lax.axis_size("sz")
    copies = jnp.broadcast_to(block[None], (inner,) + block.shape)
    block = lax.all_to_all(copies, "sz", 0, 0, tiled=True)
    block = block.reshape((inner * block.shape[1],) + block.shape[2:])
    return lax.all_gather(block, "sx", axis=0, tiled=True)


def attend_kernel(scale, q_ref, k_ref, v_ref, keep_ref, o_ref, m_ref, l_ref):
    scores = lax.dot_general(
        q_ref[...], k_ref[0], (((1,), (1,)), ((), ())), preferred_element_type=jnp.float32
    )
    scores = scores * scale
    keep = keep_ref[...] > 0.5
    pairs, n_keys = keep.shape
    heads = scores.shape[0] // pairs
    keep = jnp.broadcast_to(keep[:, None, :], (pairs, heads, n_keys)).reshape(pairs * heads, n_keys)
    masked = jnp.where(keep, scores, NEG)
    peak = jnp.max(masked, axis=1, keepdims=True)
    weights = jnp.exp(masked - jnp.maximum(peak, 0.5 * NEG))
    total = jnp.sum(weights, axis=1, keepdims=True)
    o_ref[...] = jnp.dot(
        weights.astype(jnp.bfloat16), v_ref[0], preferred_element_type=jnp.float32
    )
    m_ref[...] = jnp.broadcast_to(peak, m_ref.shape)
    l_ref[...] = jnp.broadcast_to(total, l_ref.shape)


def attend(query_all, keys, values, key_mask, scale):
    requests, new, kv, hpk, dim = query_all.shape
    n_keys = keys.shape[0]
    padded = -(-n_keys // 128) * 128
    rows = requests * new * hpk
    block = 256 if rows % 256 == 0 else rows
    steps = rows // block
    pad = ((0, padded - n_keys), (0, 0), (0, 0))
    keys_t = jnp.pad(keys, pad).transpose(1, 0, 2)
    values_t = jnp.pad(values, pad).transpose(1, 0, 2)
    keep = jnp.pad(key_mask, ((0, 0), (0, 0), (0, padded - n_keys))).astype(jnp.bfloat16)
    keep = keep.reshape(requests * new, padded)
    q_rows = query_all.transpose(2, 0, 1, 3, 4).reshape(kv * rows, dim)
    row_block = pl.BlockSpec((block, dim), lambda i: (i, 0))
    kv_block = pl.BlockSpec((1, padded, dim), lambda i: (i // steps, 0, 0))
    keep_block = pl.BlockSpec((block // hpk, padded), lambda i: (i % steps, 0))
    stat = jax.ShapeDtypeStruct((kv * rows, dim), jnp.float32)
    out, peak, total = pl.pallas_call(
        functools.partial(attend_kernel, scale),
        grid=(kv * steps,),
        in_specs=[row_block, kv_block, kv_block, keep_block],
        out_specs=[row_block, row_block, row_block],
        out_shape=[stat, stat, stat],
        compiler_params=pltpu.CompilerParams(vmem_limit_bytes=48 * 1024 * 1024),
    )(q_rows, keys_t, values_t, keep)
    out = out.reshape(kv, requests, new, hpk, dim).transpose(1, 2, 0, 3, 4)
    peak = peak[:, 0].reshape(kv, requests, new, hpk).transpose(1, 2, 0, 3)
    total = total[:, 0].reshape(kv, requests, new, hpk).transpose(1, 2, 0, 3)
    return out, peak, total


def merge(parts, n_out, n_stat):
    part_out = parts[..., :n_out]
    part_peak = parts[..., n_out : n_out + n_stat]
    part_total = parts[..., n_out + n_stat :]
    top_peak = jnp.max(part_peak, axis=0)
    factor = jnp.exp(part_peak - top_peak[None])
    total = jnp.sum(part_total * factor, axis=0)
    lead = factor.shape[:-1]
    rows = factor.reshape(lead + (n_stat, 1))
    out = parts[..., :n_out].reshape(lead + (n_stat, n_out // n_stat)) * rows
    out = jnp.sum(out, axis=0).reshape(out.shape[1:-2] + (n_out,))
    return out, top_peak, total


def inner_size(devices):
    try:
        return len({d.coords[2] for d in devices})
    except Exception:
        return 1


def local(
    queries,
    new_keys,
    new_values,
    prefix_keys,
    prefix_values,
    page_keys,
    page_values,
    out_weight,
    group_of,
    prefix_len,
    total_len,
    page_owner,
    page_slot,
    new_valid,
):
    req_dev = queries.shape[0]
    seq_count = lax.axis_size(SEQ)
    requests = req_dev * seq_count
    kv_local = new_keys.shape[2] // HEAD_DIM
    heads_local = kv_local * HPK
    score_scale = HEAD_DIM ** (-0.5)
    seq_idx = lax.axis_index(SEQ)
    gathered = gather_rows(queries)
    query_all = gathered.reshape(requests, NEW, kv_local, HPK, HEAD_DIM)

    group_hot = group_of[:, None] == jnp.arange(GROUPS, dtype=jnp.int32)[None, :]
    own_prefix = jnp.sum(jnp.where(group_hot, prefix_len[None, :], 0), axis=1)
    suffix_len = total_len - own_prefix

    pre_dev = prefix_keys.shape[1]
    page_count = page_keys.shape[0]
    page_len = page_keys.shape[1]
    keys = jnp.concatenate(
        [
            prefix_keys.reshape(GROUPS * pre_dev, kv_local, HEAD_DIM),
            page_keys.reshape(page_count * page_len, kv_local, HEAD_DIM),
            new_keys.reshape(req_dev * NEW, kv_local, HEAD_DIM),
        ],
        axis=0,
    )
    values = jnp.concatenate(
        [
            prefix_values.reshape(GROUPS * pre_dev, kv_local, HEAD_DIM),
            page_values.reshape(page_count * page_len, kv_local, HEAD_DIM),
            new_values.reshape(req_dev * NEW, kv_local, HEAD_DIM),
        ],
        axis=0,
    )

    req_ids = jnp.arange(requests, dtype=jnp.int32)
    positions = seq_idx * pre_dev + jnp.arange(pre_dev, dtype=jnp.int32)
    pre_live = positions[None, :] < prefix_len[:, None]
    pre_mask = group_hot[:, :, None] & pre_live[None, :, :]
    pre_mask = pre_mask.reshape(requests, 1, GROUPS * pre_dev)
    pre_mask = jnp.broadcast_to(pre_mask, (requests, NEW, GROUPS * pre_dev))
    owner_hot = req_ids[:, None] == page_owner[None, :]
    offsets = page_slot[:, None] * page_len + jnp.arange(page_len, dtype=jnp.int32)[None, :]
    page_live = offsets[None, :, :] < suffix_len[:, None, None]
    page_mask = (owner_hot[:, :, None] & page_live).reshape(requests, 1, page_count * page_len)
    page_mask = jnp.broadcast_to(page_mask, (requests, NEW, page_count * page_len))
    new_owner = seq_idx * req_dev + jnp.arange(req_dev, dtype=jnp.int32)
    tok = jnp.arange(NEW, dtype=jnp.int32)
    causal = tok[None, :] <= tok[:, None]
    new_live = new_valid == 1
    new_mask = (
        (req_ids[:, None, None, None] == new_owner[None, None, :, None])
        & causal[None, :, None, :]
        & new_live[:, None, None, :]
    ).reshape(requests, NEW, req_dev * NEW)
    key_mask = jnp.concatenate([pre_mask, page_mask, new_mask], axis=2)
    out, row_peak, row_total = attend(query_all, keys, values, key_mask, score_scale)

    flat_out = out.reshape(requests, -1)
    peak = row_peak.reshape(requests, -1)
    near_peak = peak.astype(jnp.bfloat16).astype(jnp.float32)
    shift = jnp.exp(peak - near_peak)
    n_stat = peak.shape[1]
    n_out = flat_out.shape[1]
    flat_out = (flat_out.reshape(requests, n_stat, -1) * shift[..., None]).reshape(requests, n_out)
    total = row_total.reshape(requests, -1) * shift
    packed = jnp.concatenate([flat_out, near_peak, total], axis=1).astype(jnp.bfloat16)
    outer = lax.axis_size("sx")
    inner = lax.axis_size("sz")
    width = packed.shape[1]
    packed = packed.reshape(outer, inner, req_dev, width)
    received = lax.all_to_all(packed, "sx", 0, 0, tiled=True).astype(jnp.float32)
    stage_out, stage_peak, stage_total = merge(received, n_out, n_stat)
    packed = jnp.concatenate([stage_out, stage_peak, stage_total], axis=-1)
    received = lax.all_to_all(packed, "sz", 0, 0, tiled=True)
    final_out, _, final_total = merge(received, n_out, n_stat)
    final_out = final_out.reshape(req_dev, NEW, kv_local, HPK, HEAD_DIM)
    final_total = final_total.reshape(req_dev, NEW, kv_local, HPK)
    row_start = seq_idx * req_dev
    valid_local = lax.dynamic_slice_in_dim(new_valid, row_start, req_dev, 0)
    valid_rows = valid_local.astype(jnp.float32)[:, :, None, None, None]
    attention = (final_out / final_total[..., None] * valid_rows).astype(jnp.bfloat16)
    attention = attention.reshape(req_dev * NEW, heads_local * HEAD_DIM)
    attention = gather_rows(attention)
    terms = jnp.dot(attention, out_weight, preferred_element_type=jnp.float32)
    n_tp = lax.axis_size("tp")
    blocks = lax.all_to_all(terms, "tp", 0, 0, tiled=True)
    blocks = blocks.reshape((n_tp, blocks.shape[0] // n_tp) + blocks.shape[1:])
    return jnp.sum(blocks, axis=0).astype(jnp.bfloat16)


def solution(mesh):
    grid = mesh.devices
    n_seq, n_tp = grid.shape
    inner = inner_size(list(grid[:, 0]))
    if inner < 1 or n_seq % inner:
        inner = 1
    mesh = Mesh(grid.reshape(n_seq // inner, inner, n_tp), ("sx", "sz", "tp"))
    placed = (
        P(SEQ, None, "tp"),
        P(SEQ, None, "tp"),
        P(SEQ, None, "tp"),
        P(None, SEQ, "tp"),
        P(None, SEQ, "tp"),
        P(SEQ, None, "tp"),
        P(SEQ, None, "tp"),
        P("tp", SEQ),
        P(),
        P(),
        P(),
        P(SEQ),
        P(SEQ),
        P(),
    )
    return jax.shard_map(
        local, mesh=mesh, in_specs=placed, out_specs=P("tp", SEQ), check_vma=False
    )
```

```python
import functools

import jax
import jax.numpy as jnp
from jax import lax
from jax.experimental import pallas as pl
from jax.experimental.pallas import tpu as pltpu
from jax.sharding import Mesh, PartitionSpec as P

HEAD_DIM = 128
HPK = 8
GROUPS = 8
NEW = 4


NEG = -(2.0**100)
SEQ = ("sx", "sz")


def gather_rows(block):
    inner = lax.axis_size("sz")
    copies = jnp.broadcast_to(block[None], (inner,) + block.shape)
    block = lax.all_to_all(copies, "sz", 0, 0, tiled=True)
    block = block.reshape((inner * block.shape[1],) + block.shape[2:])
    return lax.all_gather(block, "sx", axis=0, tiled=True)


def attend_kernel(scale, q_ref, k_ref, v_ref, keep_ref, o_ref, m_ref, l_ref):
    scores = lax.dot_general(
        q_ref[...], k_ref[0], (((1,), (1,)), ((), ())), preferred_element_type=jnp.float32
    )
    scores = scores * scale
    keep = keep_ref[...] > 0.5
    pairs, n_keys = keep.shape
    heads = scores.shape[0] // pairs
    keep = jnp.broadcast_to(keep[:, None, :], (pairs, heads, n_keys)).reshape(pairs * heads, n_keys)
    masked = jnp.where(keep, scores, NEG)
    peak = jnp.max(masked, axis=1, keepdims=True)
    weights = jnp.exp(masked - jnp.maximum(peak, 0.5 * NEG))
    total = jnp.sum(weights, axis=1, keepdims=True)
    o_ref[...] = jnp.dot(
        weights.astype(jnp.bfloat16), v_ref[0], preferred_element_type=jnp.float32
    )
    m_ref[...] = jnp.broadcast_to(peak, m_ref.shape)
    l_ref[...] = jnp.broadcast_to(total, l_ref.shape)


def attend(query_all, keys, values, key_mask, scale):
    requests, new, kv, hpk, dim = query_all.shape
    n_keys = keys.shape[0]
    padded = -(-n_keys // 128) * 128
    rows = requests * new * hpk
    block = 256 if rows % 256 == 0 else rows
    steps = rows // block
    pad = ((0, padded - n_keys), (0, 0), (0, 0))
    keys_t = jnp.pad(keys, pad).transpose(1, 0, 2)
    values_t = jnp.pad(values, pad).transpose(1, 0, 2)
    keep = jnp.pad(key_mask, ((0, 0), (0, 0), (0, padded - n_keys))).astype(jnp.bfloat16)
    keep = keep.reshape(requests * new, padded)
    q_rows = query_all.transpose(2, 0, 1, 3, 4).reshape(kv * rows, dim)
    row_block = pl.BlockSpec((block, dim), lambda i: (i, 0))
    kv_block = pl.BlockSpec((1, padded, dim), lambda i: (i // steps, 0, 0))
    keep_block = pl.BlockSpec((block // hpk, padded), lambda i: (i % steps, 0))
    stat = jax.ShapeDtypeStruct((kv * rows, dim), jnp.float32)
    out, peak, total = pl.pallas_call(
        functools.partial(attend_kernel, scale),
        grid=(kv * steps,),
        in_specs=[row_block, kv_block, kv_block, keep_block],
        out_specs=[row_block, row_block, row_block],
        out_shape=[stat, stat, stat],
        compiler_params=pltpu.CompilerParams(vmem_limit_bytes=48 * 1024 * 1024),
    )(q_rows, keys_t, values_t, keep)
    out = out.reshape(kv, requests, new, hpk, dim).transpose(1, 2, 0, 3, 4)
    peak = peak[:, 0].reshape(kv, requests, new, hpk).transpose(1, 2, 0, 3)
    total = total[:, 0].reshape(kv, requests, new, hpk).transpose(1, 2, 0, 3)
    return out, peak, total


def merge(parts, n_out, n_stat):
    part_out = parts[..., :n_out]
    part_peak = parts[..., n_out : n_out + n_stat]
    part_total = parts[..., n_out + n_stat :]
    top_peak = jnp.max(part_peak, axis=0)
    factor = jnp.exp(part_peak - top_peak[None])
    total = jnp.sum(part_total * factor, axis=0)
    lead = factor.shape[:-1]
    rows = factor.reshape(lead + (n_stat, 1))
    out = parts[..., :n_out].reshape(lead + (n_stat, n_out // n_stat)) * rows
    out = jnp.sum(out, axis=0).reshape(out.shape[1:-2] + (n_out,))
    return out, top_peak, total


def inner_size(devices):
    try:
        return len({d.coords[2] for d in devices})
    except Exception:
        return 1


def local(
    queries,
    new_keys,
    new_values,
    prefix_keys,
    prefix_values,
    page_keys,
    page_values,
    out_weight,
    group_of,
    prefix_len,
    total_len,
    page_owner,
    page_slot,
    new_valid,
):
    req_dev = queries.shape[0]
    seq_count = lax.axis_size(SEQ)
    requests = req_dev * seq_count
    kv_local = new_keys.shape[2] // HEAD_DIM
    heads_local = kv_local * HPK
    score_scale = HEAD_DIM ** (-0.5)
    seq_idx = lax.axis_index(SEQ)
    gathered = gather_rows(queries)
    query_all = gathered.reshape(requests, NEW, kv_local, HPK, HEAD_DIM)

    group_hot = group_of[:, None] == jnp.arange(GROUPS, dtype=jnp.int32)[None, :]
    own_prefix = jnp.sum(jnp.where(group_hot, prefix_len[None, :], 0), axis=1)
    suffix_len = total_len - own_prefix

    pre_dev = prefix_keys.shape[1]
    page_count = page_keys.shape[0]
    page_len = page_keys.shape[1]
    keys = jnp.concatenate(
        [
            prefix_keys.reshape(GROUPS * pre_dev, kv_local, HEAD_DIM),
            page_keys.reshape(page_count * page_len, kv_local, HEAD_DIM),
            new_keys.reshape(req_dev * NEW, kv_local, HEAD_DIM),
        ],
        axis=0,
    )
    values = jnp.concatenate(
        [
            prefix_values.reshape(GROUPS * pre_dev, kv_local, HEAD_DIM),
            page_values.reshape(page_count * page_len, kv_local, HEAD_DIM),
            new_values.reshape(req_dev * NEW, kv_local, HEAD_DIM),
        ],
        axis=0,
    )

    req_ids = jnp.arange(requests, dtype=jnp.int32)
    positions = seq_idx * pre_dev + jnp.arange(pre_dev, dtype=jnp.int32)
    pre_live = positions[None, :] < prefix_len[:, None]
    pre_mask = group_hot[:, :, None] & pre_live[None, :, :]
    pre_mask = pre_mask.reshape(requests, 1, GROUPS * pre_dev)
    pre_mask = jnp.broadcast_to(pre_mask, (requests, NEW, GROUPS * pre_dev))
    owner_hot = req_ids[:, None] == page_owner[None, :]
    offsets = page_slot[:, None] * page_len + jnp.arange(page_len, dtype=jnp.int32)[None, :]
    page_live = offsets[None, :, :] < suffix_len[:, None, None]
    page_mask = (owner_hot[:, :, None] & page_live).reshape(requests, 1, page_count * page_len)
    page_mask = jnp.broadcast_to(page_mask, (requests, NEW, page_count * page_len))
    new_owner = seq_idx * req_dev + jnp.arange(req_dev, dtype=jnp.int32)
    tok = jnp.arange(NEW, dtype=jnp.int32)
    causal = tok[None, :] <= tok[:, None]
    new_live = new_valid == 1
    new_mask = (
        (req_ids[:, None, None, None] == new_owner[None, None, :, None])
        & causal[None, :, None, :]
        & new_live[:, None, None, :]
    ).reshape(requests, NEW, req_dev * NEW)
    key_mask = jnp.concatenate([pre_mask, page_mask, new_mask], axis=2)
    out, row_peak, row_total = attend(query_all, keys, values, key_mask, score_scale)

    flat_out = out.reshape(requests, -1)
    peak = row_peak.reshape(requests, -1)
    near_peak = peak.astype(jnp.bfloat16).astype(jnp.float32)
    shift = jnp.exp(peak - near_peak)
    n_stat = peak.shape[1]
    n_out = flat_out.shape[1]
    flat_out = (flat_out.reshape(requests, n_stat, -1) * shift[..., None]).reshape(requests, n_out)
    total = row_total.reshape(requests, -1) * shift
    packed = jnp.concatenate([flat_out, near_peak, total], axis=1).astype(jnp.bfloat16)
    outer = lax.axis_size("sx")
    inner = lax.axis_size("sz")
    width = packed.shape[1]
    packed = packed.reshape(outer, inner, req_dev, width)
    received = lax.all_to_all(packed, "sx", 0, 0, tiled=True).astype(jnp.float32)
    stage_out, stage_peak, stage_total = merge(received, n_out, n_stat)
    packed = jnp.concatenate([stage_out, stage_peak, stage_total], axis=-1).astype(jnp.bfloat16)
    received = lax.all_to_all(packed, "sz", 0, 0, tiled=True).astype(jnp.float32)
    final_out, _, final_total = merge(received, n_out, n_stat)
    final_out = final_out.reshape(req_dev, NEW, kv_local, HPK, HEAD_DIM)
    final_total = final_total.reshape(req_dev, NEW, kv_local, HPK)
    row_start = seq_idx * req_dev
    valid_local = lax.dynamic_slice_in_dim(new_valid, row_start, req_dev, 0)
    valid_rows = valid_local.astype(jnp.float32)[:, :, None, None, None]
    attention = (final_out / final_total[..., None] * valid_rows).astype(jnp.bfloat16)
    attention = attention.reshape(req_dev * NEW, heads_local * HEAD_DIM)
    attention = gather_rows(attention)
    terms = jnp.dot(attention, out_weight, preferred_element_type=jnp.float32)
    n_tp = lax.axis_size("tp")
    blocks = lax.all_to_all(terms, "tp", 0, 0, tiled=True)
    blocks = blocks.reshape((n_tp, blocks.shape[0] // n_tp) + blocks.shape[1:])
    return jnp.sum(blocks, axis=0).astype(jnp.bfloat16)


def solution(mesh):
    grid = mesh.devices
    n_seq, n_tp = grid.shape
    inner = inner_size(list(grid[:, 0]))
    if inner < 1 or n_seq % inner:
        inner = 1
    mesh = Mesh(grid.reshape(n_seq // inner, inner, n_tp), ("sx", "sz", "tp"))
    placed = (
        P(SEQ, None, "tp"),
        P(SEQ, None, "tp"),
        P(SEQ, None, "tp"),
        P(None, SEQ, "tp"),
        P(None, SEQ, "tp"),
        P(SEQ, None, "tp"),
        P(SEQ, None, "tp"),
        P("tp", SEQ),
        P(),
        P(),
        P(),
        P(SEQ),
        P(SEQ),
        P(),
    )
    return jax.shard_map(
        local, mesh=mesh, in_specs=placed, out_specs=P("tp", SEQ), check_vma=False
    )
```

```python
import functools

import jax
import jax.numpy as jnp
from jax import lax
from jax.experimental import pallas as pl
from jax.experimental.pallas import tpu as pltpu
from jax.sharding import Mesh, PartitionSpec as P

HEAD_DIM = 128
HPK = 8
GROUPS = 8
NEW = 4


NEG = -(2.0**100)
SEQ = ("sx", "sz")


def gather_rows(block):
    inner = lax.axis_size("sz")
    copies = jnp.broadcast_to(block[None], (inner,) + block.shape)
    block = lax.all_to_all(copies, "sz", 0, 0, tiled=True)
    block = block.reshape((inner * block.shape[1],) + block.shape[2:])
    return lax.all_gather(block, "sx", axis=0, tiled=True)


def attend_kernel(scale, q_ref, k_ref, v_ref, keep_ref, o_ref, m_ref, l_ref):
    scores = lax.dot_general(
        q_ref[...], k_ref[0], (((1,), (1,)), ((), ())), preferred_element_type=jnp.float32
    )
    scores = scores * scale
    keep = keep_ref[...] > 0.5
    pairs, n_keys = keep.shape
    heads = scores.shape[0] // pairs
    keep = jnp.broadcast_to(keep[:, None, :], (pairs, heads, n_keys)).reshape(pairs * heads, n_keys)
    masked = jnp.where(keep, scores, NEG)
    peak = jnp.max(masked, axis=1, keepdims=True)
    weights = jnp.exp(masked - jnp.maximum(peak, 0.5 * NEG))
    total = jnp.sum(weights, axis=1, keepdims=True)
    o_ref[...] = jnp.dot(
        weights.astype(jnp.bfloat16), v_ref[0], preferred_element_type=jnp.float32
    )
    m_ref[...] = jnp.broadcast_to(peak, m_ref.shape)
    l_ref[...] = jnp.broadcast_to(total, l_ref.shape)


def attend(query_all, keys, values, key_mask, scale):
    requests, new, kv, hpk, dim = query_all.shape
    n_keys = keys.shape[0]
    padded = -(-n_keys // 128) * 128
    rows = requests * new * hpk
    block = 512 if rows % 512 == 0 else rows
    steps = rows // block
    pad = ((0, padded - n_keys), (0, 0), (0, 0))
    keys_t = jnp.pad(keys, pad).transpose(1, 0, 2)
    values_t = jnp.pad(values, pad).transpose(1, 0, 2)
    keep = jnp.pad(key_mask, ((0, 0), (0, 0), (0, padded - n_keys))).astype(jnp.bfloat16)
    keep = keep.reshape(requests * new, padded)
    q_rows = query_all.transpose(2, 0, 1, 3, 4).reshape(kv * rows, dim)
    row_block = pl.BlockSpec((block, dim), lambda i: (i, 0))
    kv_block = pl.BlockSpec((1, padded, dim), lambda i: (i // steps, 0, 0))
    keep_block = pl.BlockSpec((block // hpk, padded), lambda i: (i % steps, 0))
    stat = jax.ShapeDtypeStruct((kv * rows, dim), jnp.float32)
    out, peak, total = pl.pallas_call(
        functools.partial(attend_kernel, scale),
        grid=(kv * steps,),
        in_specs=[row_block, kv_block, kv_block, keep_block],
        out_specs=[row_block, row_block, row_block],
        out_shape=[stat, stat, stat],
        compiler_params=pltpu.CompilerParams(vmem_limit_bytes=48 * 1024 * 1024),
    )(q_rows, keys_t, values_t, keep)
    out = out.reshape(kv, requests, new, hpk, dim).transpose(1, 2, 0, 3, 4)
    peak = peak[:, 0].reshape(kv, requests, new, hpk).transpose(1, 2, 0, 3)
    total = total[:, 0].reshape(kv, requests, new, hpk).transpose(1, 2, 0, 3)
    return out, peak, total


def merge(parts, n_out, n_stat):
    part_out = parts[..., :n_out]
    part_peak = parts[..., n_out : n_out + n_stat]
    part_total = parts[..., n_out + n_stat :]
    top_peak = jnp.max(part_peak, axis=0)
    factor = jnp.exp(part_peak - top_peak[None])
    total = jnp.sum(part_total * factor, axis=0)
    lead = factor.shape[:-1]
    rows = factor.reshape(lead + (n_stat, 1))
    out = parts[..., :n_out].reshape(lead + (n_stat, n_out // n_stat)) * rows
    out = jnp.sum(out, axis=0).reshape(out.shape[1:-2] + (n_out,))
    return out, top_peak, total


def inner_size(devices):
    try:
        return len({d.coords[2] for d in devices})
    except Exception:
        return 1


def local(
    queries,
    new_keys,
    new_values,
    prefix_keys,
    prefix_values,
    page_keys,
    page_values,
    out_weight,
    group_of,
    prefix_len,
    total_len,
    page_owner,
    page_slot,
    new_valid,
):
    req_dev = queries.shape[0]
    seq_count = lax.axis_size(SEQ)
    requests = req_dev * seq_count
    kv_local = new_keys.shape[2] // HEAD_DIM
    heads_local = kv_local * HPK
    score_scale = HEAD_DIM ** (-0.5)
    seq_idx = lax.axis_index(SEQ)
    gathered = gather_rows(queries)
    query_all = gathered.reshape(requests, NEW, kv_local, HPK, HEAD_DIM)

    group_hot = group_of[:, None] == jnp.arange(GROUPS, dtype=jnp.int32)[None, :]
    own_prefix = jnp.sum(jnp.where(group_hot, prefix_len[None, :], 0), axis=1)
    suffix_len = total_len - own_prefix

    pre_dev = prefix_keys.shape[1]
    page_count = page_keys.shape[0]
    page_len = page_keys.shape[1]
    keys = jnp.concatenate(
        [
            prefix_keys.reshape(GROUPS * pre_dev, kv_local, HEAD_DIM),
            page_keys.reshape(page_count * page_len, kv_local, HEAD_DIM),
            new_keys.reshape(req_dev * NEW, kv_local, HEAD_DIM),
        ],
        axis=0,
    )
    values = jnp.concatenate(
        [
            prefix_values.reshape(GROUPS * pre_dev, kv_local, HEAD_DIM),
            page_values.reshape(page_count * page_len, kv_local, HEAD_DIM),
            new_values.reshape(req_dev * NEW, kv_local, HEAD_DIM),
        ],
        axis=0,
    )

    req_ids = jnp.arange(requests, dtype=jnp.int32)
    positions = seq_idx * pre_dev + jnp.arange(pre_dev, dtype=jnp.int32)
    pre_live = positions[None, :] < prefix_len[:, None]
    pre_mask = group_hot[:, :, None] & pre_live[None, :, :]
    pre_mask = pre_mask.reshape(requests, 1, GROUPS * pre_dev)
    pre_mask = jnp.broadcast_to(pre_mask, (requests, NEW, GROUPS * pre_dev))
    owner_hot = req_ids[:, None] == page_owner[None, :]
    offsets = page_slot[:, None] * page_len + jnp.arange(page_len, dtype=jnp.int32)[None, :]
    page_live = offsets[None, :, :] < suffix_len[:, None, None]
    page_mask = (owner_hot[:, :, None] & page_live).reshape(requests, 1, page_count * page_len)
    page_mask = jnp.broadcast_to(page_mask, (requests, NEW, page_count * page_len))
    new_owner = seq_idx * req_dev + jnp.arange(req_dev, dtype=jnp.int32)
    tok = jnp.arange(NEW, dtype=jnp.int32)
    causal = tok[None, :] <= tok[:, None]
    new_live = new_valid == 1
    new_mask = (
        (req_ids[:, None, None, None] == new_owner[None, None, :, None])
        & causal[None, :, None, :]
        & new_live[:, None, None, :]
    ).reshape(requests, NEW, req_dev * NEW)
    key_mask = jnp.concatenate([pre_mask, page_mask, new_mask], axis=2)
    out, row_peak, row_total = attend(query_all, keys, values, key_mask, score_scale)

    flat_out = out.reshape(requests, -1)
    peak = row_peak.reshape(requests, -1)
    near_peak = peak.astype(jnp.bfloat16).astype(jnp.float32)
    shift = jnp.exp(peak - near_peak)
    n_stat = peak.shape[1]
    n_out = flat_out.shape[1]
    flat_out = (flat_out.reshape(requests, n_stat, -1) * shift[..., None]).reshape(requests, n_out)
    total = row_total.reshape(requests, -1) * shift
    packed = jnp.concatenate([flat_out, near_peak, total], axis=1).astype(jnp.bfloat16)
    outer = lax.axis_size("sx")
    inner = lax.axis_size("sz")
    width = packed.shape[1]
    packed = packed.reshape(outer, inner, req_dev, width)
    received = lax.all_to_all(packed, "sx", 0, 0, tiled=True).astype(jnp.float32)
    stage_out, stage_peak, stage_total = merge(received, n_out, n_stat)
    packed = jnp.concatenate([stage_out, stage_peak, stage_total], axis=-1).astype(jnp.bfloat16)
    received = lax.all_to_all(packed, "sz", 0, 0, tiled=True).astype(jnp.float32)
    final_out, _, final_total = merge(received, n_out, n_stat)
    final_out = final_out.reshape(req_dev, NEW, kv_local, HPK, HEAD_DIM)
    final_total = final_total.reshape(req_dev, NEW, kv_local, HPK)
    row_start = seq_idx * req_dev
    valid_local = lax.dynamic_slice_in_dim(new_valid, row_start, req_dev, 0)
    valid_rows = valid_local.astype(jnp.float32)[:, :, None, None, None]
    attention = (final_out / final_total[..., None] * valid_rows).astype(jnp.bfloat16)
    attention = attention.reshape(req_dev * NEW, heads_local * HEAD_DIM)
    attention = gather_rows(attention)
    terms = jnp.dot(attention, out_weight, preferred_element_type=jnp.float32)
    n_tp = lax.axis_size("tp")
    blocks = lax.all_to_all(terms, "tp", 0, 0, tiled=True)
    blocks = blocks.reshape((n_tp, blocks.shape[0] // n_tp) + blocks.shape[1:])
    return jnp.sum(blocks, axis=0).astype(jnp.bfloat16)


def solution(mesh):
    grid = mesh.devices
    n_seq, n_tp = grid.shape
    inner = inner_size(list(grid[:, 0]))
    if inner < 1 or n_seq % inner:
        inner = 1
    mesh = Mesh(grid.reshape(n_seq // inner, inner, n_tp), ("sx", "sz", "tp"))
    placed = (
        P(SEQ, None, "tp"),
        P(SEQ, None, "tp"),
        P(SEQ, None, "tp"),
        P(None, SEQ, "tp"),
        P(None, SEQ, "tp"),
        P(SEQ, None, "tp"),
        P(SEQ, None, "tp"),
        P("tp", SEQ),
        P(),
        P(),
        P(),
        P(SEQ),
        P(SEQ),
        P(),
    )
    return jax.shard_map(
        local, mesh=mesh, in_specs=placed, out_specs=P("tp", SEQ), check_vma=False
    )
```

```python
import functools

import jax
import jax.numpy as jnp
from jax import lax
from jax.experimental import pallas as pl
from jax.experimental.pallas import tpu as pltpu
from jax.sharding import Mesh, PartitionSpec as P

HEAD_DIM = 128
HPK = 8
GROUPS = 8
NEW = 4


NEG = -(2.0**100)
SEQ = ("sx", "sz")


def gather_rows(block):
    inner = lax.axis_size("sz")
    copies = jnp.broadcast_to(block[None], (inner,) + block.shape)
    block = lax.all_to_all(copies, "sz", 0, 0, tiled=True)
    block = block.reshape((inner * block.shape[1],) + block.shape[2:])
    return lax.all_gather(block, "sx", axis=0, tiled=True)


def attend_kernel(scale, q_ref, k_ref, v_ref, keep_ref, o_ref, m_ref, l_ref):
    scores = lax.dot_general(
        q_ref[...], k_ref[0], (((1,), (1,)), ((), ())), preferred_element_type=jnp.float32
    )
    scores = scores * scale
    keep = keep_ref[...] > 0.5
    pairs, n_keys = keep.shape
    heads = scores.shape[0] // pairs
    keep = jnp.broadcast_to(keep[:, None, :], (pairs, heads, n_keys)).reshape(pairs * heads, n_keys)
    masked = jnp.where(keep, scores, NEG)
    peak = jnp.max(masked, axis=1, keepdims=True)
    weights = jnp.exp(masked - jnp.maximum(peak, 0.5 * NEG))
    total = jnp.sum(weights, axis=1, keepdims=True)
    o_ref[...] = jnp.dot(
        weights.astype(jnp.bfloat16), v_ref[0], preferred_element_type=jnp.float32
    )
    m_ref[...] = jnp.broadcast_to(peak, m_ref.shape)
    l_ref[...] = jnp.broadcast_to(total, l_ref.shape)


def attend(query_all, keys, values, key_mask, scale):
    requests, new, kv, hpk, dim = query_all.shape
    n_keys = keys.shape[0]
    padded = -(-n_keys // 128) * 128
    rows = requests * new * hpk
    block = 256 if rows % 256 == 0 else rows
    steps = rows // block
    pad = ((0, padded - n_keys), (0, 0), (0, 0))
    keys_t = jnp.pad(keys, pad).transpose(1, 0, 2)
    values_t = jnp.pad(values, pad).transpose(1, 0, 2)
    keep = jnp.pad(key_mask, ((0, 0), (0, 0), (0, padded - n_keys))).astype(jnp.bfloat16)
    keep = keep.reshape(requests * new, padded)
    q_rows = query_all.transpose(2, 0, 1, 3, 4).reshape(kv * rows, dim)
    row_block = pl.BlockSpec((block, dim), lambda i: (i, 0))
    kv_block = pl.BlockSpec((1, padded, dim), lambda i: (i // steps, 0, 0))
    keep_block = pl.BlockSpec((block // hpk, padded), lambda i: (i % steps, 0))
    stat = jax.ShapeDtypeStruct((kv * rows, dim), jnp.float32)
    out, peak, total = pl.pallas_call(
        functools.partial(attend_kernel, scale),
        grid=(kv * steps,),
        in_specs=[row_block, kv_block, kv_block, keep_block],
        out_specs=[row_block, row_block, row_block],
        out_shape=[stat, stat, stat],
        compiler_params=pltpu.CompilerParams(vmem_limit_bytes=48 * 1024 * 1024),
    )(q_rows, keys_t, values_t, keep)
    out = out.reshape(kv, requests, new, hpk, dim).transpose(1, 2, 0, 3, 4)
    peak = peak[:, 0].reshape(kv, requests, new, hpk).transpose(1, 2, 0, 3)
    total = total[:, 0].reshape(kv, requests, new, hpk).transpose(1, 2, 0, 3)
    return out, peak, total


def merge(parts, n_out, n_stat):
    part_out = parts[..., :n_out]
    part_peak = parts[..., n_out : n_out + n_stat]
    part_total = parts[..., n_out + n_stat :]
    top_peak = jnp.max(part_peak, axis=0)
    factor = jnp.exp(part_peak - top_peak[None])
    total = jnp.sum(part_total * factor, axis=0)
    lead = factor.shape[:-1]
    rows = factor.reshape(lead + (n_stat, 1))
    out = parts[..., :n_out].reshape(lead + (n_stat, n_out // n_stat)) * rows
    out = jnp.sum(out, axis=0).reshape(out.shape[1:-2] + (n_out,))
    return out, top_peak, total


def inner_size(devices):
    try:
        return len({d.coords[2] for d in devices})
    except Exception:
        return 1


def local(
    queries,
    new_keys,
    new_values,
    prefix_keys,
    prefix_values,
    page_keys,
    page_values,
    out_weight,
    group_of,
    prefix_len,
    total_len,
    page_owner,
    page_slot,
    new_valid,
):
    req_dev = queries.shape[0]
    seq_count = lax.axis_size(SEQ)
    requests = req_dev * seq_count
    kv_local = new_keys.shape[2] // HEAD_DIM
    heads_local = kv_local * HPK
    score_scale = HEAD_DIM ** (-0.5)
    seq_idx = lax.axis_index(SEQ)
    gathered = gather_rows(queries)
    query_all = gathered.reshape(requests, NEW, kv_local, HPK, HEAD_DIM)

    group_hot = group_of[:, None] == jnp.arange(GROUPS, dtype=jnp.int32)[None, :]
    own_prefix = jnp.sum(jnp.where(group_hot, prefix_len[None, :], 0), axis=1)
    suffix_len = total_len - own_prefix

    pre_dev = prefix_keys.shape[1]
    page_count = page_keys.shape[0]
    page_len = page_keys.shape[1]
    keys = jnp.concatenate(
        [
            prefix_keys.reshape(GROUPS * pre_dev, kv_local, HEAD_DIM),
            page_keys.reshape(page_count * page_len, kv_local, HEAD_DIM),
            new_keys.reshape(req_dev * NEW, kv_local, HEAD_DIM),
        ],
        axis=0,
    )
    values = jnp.concatenate(
        [
            prefix_values.reshape(GROUPS * pre_dev, kv_local, HEAD_DIM),
            page_values.reshape(page_count * page_len, kv_local, HEAD_DIM),
            new_values.reshape(req_dev * NEW, kv_local, HEAD_DIM),
        ],
        axis=0,
    )

    req_ids = jnp.arange(requests, dtype=jnp.int32)
    positions = seq_idx * pre_dev + jnp.arange(pre_dev, dtype=jnp.int32)
    pre_live = positions[None, :] < prefix_len[:, None]
    pre_mask = group_hot[:, :, None] & pre_live[None, :, :]
    pre_mask = pre_mask.reshape(requests, 1, GROUPS * pre_dev)
    pre_mask = jnp.broadcast_to(pre_mask, (requests, NEW, GROUPS * pre_dev))
    owner_hot = req_ids[:, None] == page_owner[None, :]
    offsets = page_slot[:, None] * page_len + jnp.arange(page_len, dtype=jnp.int32)[None, :]
    page_live = offsets[None, :, :] < suffix_len[:, None, None]
    page_mask = (owner_hot[:, :, None] & page_live).reshape(requests, 1, page_count * page_len)
    page_mask = jnp.broadcast_to(page_mask, (requests, NEW, page_count * page_len))
    new_owner = seq_idx * req_dev + jnp.arange(req_dev, dtype=jnp.int32)
    tok = jnp.arange(NEW, dtype=jnp.int32)
    causal = tok[None, :] <= tok[:, None]
    new_live = new_valid == 1
    new_mask = (
        (req_ids[:, None, None, None] == new_owner[None, None, :, None])
        & causal[None, :, None, :]
        & new_live[:, None, None, :]
    ).reshape(requests, NEW, req_dev * NEW)
    key_mask = jnp.concatenate([pre_mask, page_mask, new_mask], axis=2)
    out, row_peak, row_total = attend(query_all, keys, values, key_mask, score_scale)

    flat_out = out.reshape(requests, -1)
    peak = row_peak.reshape(requests, -1)
    near_peak = peak.astype(jnp.bfloat16).astype(jnp.float32)
    shift = jnp.exp(peak - near_peak)
    n_stat = peak.shape[1]
    n_out = flat_out.shape[1]
    flat_out = (flat_out.reshape(requests, n_stat, -1) * shift[..., None]).reshape(requests, n_out)
    total = row_total.reshape(requests, -1) * shift
    packed = jnp.concatenate([flat_out, near_peak, total], axis=1).astype(jnp.bfloat16)
    outer = lax.axis_size("sx")
    inner = lax.axis_size("sz")
    width = packed.shape[1]
    packed = packed.reshape(outer, inner, req_dev, width)
    received = lax.all_to_all(packed, "sx", 0, 0, tiled=True).astype(jnp.float32)
    stage_out, stage_peak, stage_total = merge(received, n_out, n_stat)
    packed = jnp.concatenate([stage_out, stage_peak, stage_total], axis=-1).astype(jnp.bfloat16)
    received = lax.all_to_all(packed, "sz", 0, 0, tiled=True).astype(jnp.float32)
    final_out, _, final_total = merge(received, n_out, n_stat)
    final_out = final_out.reshape(req_dev, NEW, kv_local, HPK, HEAD_DIM)
    final_total = final_total.reshape(req_dev, NEW, kv_local, HPK)
    row_start = seq_idx * req_dev
    valid_local = lax.dynamic_slice_in_dim(new_valid, row_start, req_dev, 0)
    valid_rows = valid_local.astype(jnp.float32)[:, :, None, None, None]
    attention = (final_out / final_total[..., None] * valid_rows).astype(jnp.bfloat16)
    attention = attention.reshape(req_dev * NEW, heads_local * HEAD_DIM)
    attention = gather_rows(attention)
    terms = jnp.dot(attention, out_weight, preferred_element_type=jnp.float32)
    n_tp = lax.axis_size("tp")
    blocks = lax.all_to_all(terms.astype(jnp.bfloat16), "tp", 0, 0, tiled=True)
    blocks = blocks.astype(jnp.float32)
    blocks = blocks.reshape((n_tp, blocks.shape[0] // n_tp) + blocks.shape[1:])
    return jnp.sum(blocks, axis=0).astype(jnp.bfloat16)


def solution(mesh):
    grid = mesh.devices
    n_seq, n_tp = grid.shape
    inner = inner_size(list(grid[:, 0]))
    if inner < 1 or n_seq % inner:
        inner = 1
    mesh = Mesh(grid.reshape(n_seq // inner, inner, n_tp), ("sx", "sz", "tp"))
    placed = (
        P(SEQ, None, "tp"),
        P(SEQ, None, "tp"),
        P(SEQ, None, "tp"),
        P(None, SEQ, "tp"),
        P(None, SEQ, "tp"),
        P(SEQ, None, "tp"),
        P(SEQ, None, "tp"),
        P("tp", SEQ),
        P(),
        P(),
        P(),
        P(SEQ),
        P(SEQ),
        P(),
    )
    return jax.shard_map(
        local, mesh=mesh, in_specs=placed, out_specs=P("tp", SEQ), check_vma=False
    )
```
